128 devices in a mesh: visit: 8 (over y, core), patch: 16 (over x, z).
Axes of the slice: x: 4, y: 4, z: 4, core: 2. Of those that a mesh axis runs over, the one named last changes fastest.
Arguments:
- pieces: float32 [1024, 512, 512], P(('visit', 'patch')), may hold values from -60 to 60
- ref_patch: float32 [16, 512, 512], P('patch', 'visit'), may hold values from -6 to 6
- piece_patch: int32 [1024], P(('visit', 'patch')), may hold values from 0 to 15, as said below
- piece_visit: int32 [1024], P(('visit', 'patch')), may hold values from 0 to 3, as said below
- anchors: int32 [1024, 2], P(('visit', 'patch')), may hold values from 0 to 3584
- shifts: int32 [1024, 2], P(('visit', 'patch')), may hold values from -2 to 2
- phases: float32 [1024, 2], P(('visit', 'patch')), may hold values from 0 to 1
Outputs:
- matched: float32 [1024, 512, 512], P(('visit', 'patch'))
- coefficients: float32 [32, 17, 17], P('visit')
The draws below stay inside these ranges and needn't reach their ends.
Inputs may be any that keep to these rules, and one draw needn't show every extreme that they name: `piece_patch`: among the 8 pieces of one device at most 2 name the same patch; for each index of the visit axis one patch, drawn from the seed, is named by exactly 2 pieces of every device of that index. `piece_visit`: among the 8 pieces of one device each value occurs exactly 8 / 4 times.
All inputs are finite; a program needn't handle non-finite values.
Results may differ from the reference program's by a relative error of at most 0.0003.
Values sent between devices are 32-bit elements; how exact they have to be, the bound alone decides.
No kernel may reach another device: no remote copies, remote signals or barrier semaphores. Data moves between devices by JAX's collectives and lax.ppermute only.
A program may use at most 192 MiB of HBM per device.

```python
import jax
import jax.numpy as jnp
from jax import lax

PIX = 512
PIECE_DEV = 8
VIS_DEV = 4
CAP = 2
TERMS = 17
TILE = 4096
PATCHES = 16
VISITS = 32
PIECES = 1024


def visit_layout(key):
    base_key = jax.random.fold_in(key, 7101)
    block_total = PIECES // PIECE_DEV

    def one_block(block_id):
        sub_key = jax.random.fold_in(base_key, block_id)
        ordering = jax.random.permutation(sub_key, PIECE_DEV)
        return (ordering % VIS_DEV).astype(jnp.int32)
    return jax.vmap(one_block)(jnp.arange(block_total, dtype=jnp.int32)).reshape(PIECES).astype(jnp.int32)


def draw_piece_visit(key, part):
    return visit_layout(key)


def draw_piece_patch(key, part):
    base_key = jax.random.fold_in(key, 7202)
    row_total = PIECES // (PIECE_DEV * PATCHES)
    block_total = PIECES // PIECE_DEV
    hot_all = jax.random.randint(jax.random.fold_in(base_key, 1), (row_total,), 0, PATCHES).astype(jnp.int32)

    def one_block(block_id):
        sub_key = jax.random.fold_in(base_key, block_id + 17)
        hot_patch = hot_all[block_id // PATCHES]
        others = jax.random.permutation(jax.random.fold_in(sub_key, 1), PATCHES - 1).astype(jnp.int32)
        others = others + (others >= hot_patch).astype(jnp.int32)
        start_shift = jax.random.randint(jax.random.fold_in(sub_key, 2), (), 0, CAP).astype(jnp.int32)
        rank_list = jnp.arange(PIECE_DEV, dtype=jnp.int32) - CAP
        pick_index = jnp.clip((rank_list + start_shift) // CAP, 0, PATCHES - 2)
        labels = jnp.where(rank_list < 0, hot_patch, others[pick_index])
        shuffle = jax.random.permutation(jax.random.fold_in(sub_key, 3), PIECE_DEV)
        return labels[shuffle].astype(jnp.int32)
    return jax.vmap(one_block)(jnp.arange(block_total, dtype=jnp.int32)).reshape(PIECES).astype(jnp.int32)


def draw_pieces(key, part):
    local_visit = visit_layout(key)
    block_of = jnp.arange(PIECES, dtype=jnp.int32) // PIECE_DEV
    column = (block_of % PATCHES).astype(jnp.float32)
    visit_id = block_of // PATCHES * VIS_DEV + local_visit
    level_key = jax.random.fold_in(key, 7303)
    keys_all = jax.random.split(level_key, 6)
    levels = jax.random.uniform(keys_all[0], (VISITS,), jnp.float32, -2.0, 2.0)
    rise_factor = 1.0 + 2.0 * column / (PATCHES - 1)
    noise_field = jax.random.normal(keys_all[1], (PIECES, PIX, PIX), jnp.float32)
    row_scale = jnp.exp(jax.random.uniform(keys_all[2], (PIECES, PIX), jnp.float32, -0.6931472, 1.6094379))
    amplitude = jax.random.uniform(keys_all[3], (VISITS,), jnp.float32, 0.5, 1.5)
    row_order = jax.random.randint(keys_all[4], (VISITS,), 0, TERMS).astype(jnp.float32)
    col_order = jax.random.randint(keys_all[5], (VISITS,), 0, TERMS).astype(jnp.float32)
    grid_coord = (2.0 * jnp.arange(PIX).astype(jnp.float32) + 1.0) / PIX - 1.0
    angles = jnp.arccos(grid_coord)
    row_wave = jnp.cos(row_order[visit_id][:, None] * angles[None, :])
    col_wave = jnp.cos(col_order[visit_id][:, None] * angles[None, :])
    smooth = levels[visit_id][:, None, None] + amplitude[visit_id][:, None, None] * row_wave[:, :, None] * col_wave[:, None, :]
    return (noise_field * row_scale[:, :, None] + rise_factor[:, None, None] * smooth).astype(jnp.float32)


def plant(array, stream_key, least, largest):
    index_at = [jax.random.randint(jax.random.fold_in(stream_key, axis), (), 0, length) for axis, length in enumerate(array.shape)]
    widest = array.shape.index(max(array.shape))
    neighbour = index_at[:widest] + [(index_at[widest] + 1) % array.shape[widest]] + index_at[widest + 1:]
    return array.at[tuple(index_at)].set(least).at[tuple(neighbour)].set(largest)


def block_levels(stream_key, shape, cuts, least, largest):
    level, own = 1.0, jax.random.fold_in(stream_key, 6)
    for dim, shards_of in cuts:
        heights = jnp.exp(jax.random.uniform(jax.random.fold_in(own, dim), (shards_of,), jnp.float32, least / len(cuts), largest / len(cuts)))
        level = level * jnp.repeat(heights, shape[dim] // shards_of).reshape([-1 if axis == dim else 1 for axis in range(len(shape))])
    return level


def noise(key, dims, spread, limit, cuts=(), kind=jnp.bfloat16):
    level = block_levels(key, dims, cuts, -0.22, 0.18) if cuts else 1.0
    drawn = jax.random.normal(key, dims, jnp.float32) * spread * level
    return jnp.minimum(jnp.maximum(drawn, -limit), limit).astype(kind)


def setup_inputs(seed: int = 0) -> dict:
    key_list = jax.random.split(jax.random.key(seed), 8)
    pieces = draw_pieces(jax.random.fold_in(key_list[7], 71), 0)
    ref_patch = noise(key_list[1], (PATCHES, PIX, PIX), 1.0, 6.0, ((0, 16), (1, 8)), jnp.float32)
    piece_patch = draw_piece_patch(jax.random.fold_in(key_list[7], 71), 0)
    piece_visit = draw_piece_visit(jax.random.fold_in(key_list[7], 71), 0)
    anchors = plant(jax.random.randint(key_list[4], (PIECES, 2), 0, TILE - PIX + 1), jax.random.fold_in(key_list[4], 1), 0, TILE - PIX).astype(jnp.int32)
    shifts = plant(jax.random.randint(key_list[5], (PIECES, 2), -2, 3), jax.random.fold_in(key_list[5], 1), -2, 2).astype(jnp.int32)
    phases = jnp.clip(1.0 * jax.random.uniform(key_list[6], (PIECES, 2), jnp.float32) ** block_levels(key_list[6], (PIECES, 2), ((0, 128),), -0.2, 0.2), 0.0, 1.0)
    return {"pieces": pieces, "ref_patch": ref_patch, "piece_patch": piece_patch, "piece_visit": piece_visit, "anchors": anchors, "shifts": shifts, "phases": phases}


exact_mode = lax.Precision.HIGHEST


def lanczos_matrix(band_shift, sub_phase, side_len):
    positions = jnp.arange(side_len, dtype=jnp.int32)
    offset = (positions[:, None] + band_shift - positions[None, :]).astype(sub_phase.dtype) + sub_phase
    weight = jnp.sinc(offset) * jnp.sinc(offset / 3.0)
    return jnp.where(jnp.abs(offset) < 3.0, weight, jnp.zeros_like(weight))


def chebyshev_rows(first_pixel, side_len):
    pixels = (first_pixel + jnp.arange(side_len, dtype=jnp.int32)).astype(jnp.float32)
    coordinate = (2.0 * pixels + 1.0) / TILE - 1.0
    orders = jnp.arange(TERMS, dtype=jnp.int32).astype(jnp.float32)
    return jnp.cos(orders[:, None] * jnp.arccos(coordinate)[None, :])


def warp_piece(slab_image, row_shift, col_shift, row_phase, col_phase):
    side_len = slab_image.shape[0]
    left_matrix = lanczos_matrix(row_shift, row_phase, side_len)
    right_matrix = lanczos_matrix(col_shift, col_phase, side_len)
    middle = jnp.dot(left_matrix, slab_image, precision=exact_mode)
    return jnp.dot(middle, right_matrix.T, precision=exact_mode)


def reference(pieces, ref_patch, piece_patch, piece_visit, anchors, shifts, phases):
    per_visit = PATCHES * PIECE_DEV // VIS_DEV
    row_of = jnp.arange(PIECES, dtype=jnp.int32) // (PIECE_DEV * PATCHES)
    visit_of = (row_of * VIS_DEV + piece_visit).astype(jnp.int32)

    def difference(inputs):
        slab_image, patch_id, band_pair, phase_pair = inputs
        warped = warp_piece(slab_image, band_pair[0], band_pair[1], phase_pair[0], phase_pair[1])
        return warped - lax.dynamic_index_in_dim(ref_patch, patch_id, 0, keepdims=False)

    diffs = lax.map(difference, (pieces, piece_patch, shifts, phases))

    def project(inputs):
        diff_image, anchor_pair = inputs
        row_basis = chebyshev_rows(anchor_pair[0], PIX)
        col_basis = chebyshev_rows(anchor_pair[1], PIX)
        middle = jnp.dot(row_basis, diff_image, precision=exact_mode)
        return jnp.dot(middle, col_basis.T, precision=exact_mode)

    partial_value = lax.map(project, (diffs, anchors))
    totals = jax.ops.segment_sum(partial_value, visit_of, num_segments=VISITS)
    coefficients = totals / (per_visit * PIX * PIX)

    def subtract_fit(inputs):
        diff_image, anchor_pair, visit_id = inputs
        row_basis = chebyshev_rows(anchor_pair[0], PIX)
        col_basis = chebyshev_rows(anchor_pair[1], PIX)
        chosen = lax.dynamic_index_in_dim(coefficients, visit_id, 0, keepdims=False)
        middle = jnp.dot(row_basis.T, chosen, precision=exact_mode)
        return diff_image - jnp.dot(middle, col_basis, precision=exact_mode)

    matched = lax.map(subtract_fit, (diffs, anchors, visit_of))
    return matched, coefficients
```

```python
import jax
import jax.numpy as jnp
from jax import lax
from jax.sharding import PartitionSpec as P

VIS_DEV = 4
TERMS = 17
TILE = 4096
TAPS = 6


exact_mode = lax.Precision.HIGHEST
warp_mode = lax.Precision.HIGH


def tap_weights(sub_phase):
    distance = jnp.arange(-3, 3, dtype=jnp.int32)
    offset = distance.astype(sub_phase.dtype)[None, :] + sub_phase[:, None]
    weight = jnp.sinc(offset) * jnp.sinc(offset / 3.0)
    return jnp.where(jnp.abs(offset) < 3.0, weight, jnp.zeros_like(weight))


def lanczos_batch(band_shift, sub_phase, side_len):
    positions = jnp.arange(side_len, dtype=jnp.int32)
    whole = positions[None, :, None] + band_shift[:, None, None] - positions[None, None, :]
    weights = tap_weights(sub_phase)
    matrix = jnp.zeros(whole.shape, sub_phase.dtype)
    for tap in range(TAPS):
        matrix = jnp.where(whole == tap - 3, weights[:, tap][:, None, None], matrix)
    return matrix


def warp_batch(slab_images, row_shift, col_shift, row_phase, col_phase):
    side_len = slab_images.shape[1]
    left_matrix = lanczos_batch(row_shift, row_phase, side_len)
    middle = jnp.einsum("kia,kab->kib", left_matrix, slab_images, precision=warp_mode)
    right_matrix = lanczos_batch(col_shift, col_phase, side_len)
    return jnp.einsum("kib,kjb->kij", middle, right_matrix, precision=warp_mode)


def chebyshev_rows(first_pixel, side_len):
    pixels = (first_pixel + jnp.arange(side_len, dtype=jnp.int32)).astype(jnp.float32)
    coordinate = (2.0 * pixels + 1.0) / TILE - 1.0
    orders = jnp.arange(TERMS, dtype=jnp.int32).astype(jnp.float32)
    return jnp.cos(orders[:, None] * jnp.arccos(coordinate)[None, :])


def basis_pair(anchor_pairs, side_len):
    row_basis = jax.vmap(lambda first_pixel: chebyshev_rows(first_pixel, side_len))(
        anchor_pairs[:, 0]
    )
    col_basis = jax.vmap(lambda first_pixel: chebyshev_rows(first_pixel, side_len))(
        anchor_pairs[:, 1]
    )
    return (row_basis, col_basis)


def project_terms(differences, row_basis, col_basis):
    middle = jnp.einsum("mtp,mpq->mtq", row_basis, differences, precision=exact_mode)
    return jnp.einsum("mtq,muq->mtu", middle, col_basis, precision=exact_mode)


def butterfly_sum(value, axis_name):
    count = lax.axis_size(axis_name)
    stride = 1
    while stride < count:
        pairs = [(i, i ^ stride) for i in range(count)]
        value = value + lax.ppermute(value, axis_name, pairs)
        stride *= 2
    return value


def body(pieces, ref_patch, piece_patch, piece_visit, anchors, shifts, phases):
    piece_count = pieces.shape[0]
    side_len = pieces.shape[1]
    patch_count = lax.axis_size("patch")
    gathered = lax.all_gather(ref_patch, ("patch", "visit"), axis=0, tiled=True)
    ref_block = gathered.reshape(patch_count, side_len, side_len)
    visit_slots = jnp.arange(VIS_DEV, dtype=jnp.int32)
    own_onehot = (piece_visit[:, None] == visit_slots[None, :]).astype(jnp.float32)
    warped_all = warp_batch(pieces, shifts[:, 0], shifts[:, 1], phases[:, 0], phases[:, 1])
    own_diffs = warped_all - jnp.take(ref_block, piece_patch, axis=0)
    row_basis, col_basis = basis_pair(anchors, side_len)
    partial_value = project_terms(own_diffs, row_basis, col_basis)
    local_sums = jnp.einsum("kv,ktu->vtu", own_onehot, partial_value, precision=exact_mode)
    totals = butterfly_sum(local_sums, "patch")
    coefficients = totals / float(patch_count * (piece_count // VIS_DEV) * side_len * side_len)
    chosen = jnp.take(coefficients, piece_visit, axis=0)
    middle = jnp.einsum("ktp,ktu->kpu", row_basis, chosen, precision=warp_mode)
    fitted = jnp.einsum("kpu,kuq->kpq", middle, col_basis, precision=warp_mode)
    return (own_diffs - fitted, coefficients)


def solution(mesh):
    return jax.shard_map(
        body,
        mesh=mesh,
        in_specs=(
            P(("visit", "patch"), None, None),
            P("patch", "visit", None),
            P(("visit", "patch")),
            P(("visit", "patch")),
            P(("visit", "patch"), None),
            P(("visit", "patch"), None),
            P(("visit", "patch"), None),
        ),
        out_specs=(P(("visit", "patch"), None, None), P("visit", None, None)),
        check_vma=False,
    )
```

```python
import jax
import jax.numpy as jnp
from jax import lax
from jax.sharding import Mesh
from jax.sharding import PartitionSpec as P

VIS_DEV = 4
TERMS = 17
TILE = 4096
TAPS = 6

VISIT_PARTS = ("vy", "vc")
PATCH_PARTS = ("px", "pz")
PIECE_AXES = VISIT_PARTS + PATCH_PARTS

exact_mode = lax.Precision.HIGHEST
warp_mode = lax.Precision.HIGH


def tap_weights(sub_phase):
    distance = jnp.arange(-3, 3, dtype=jnp.int32)
    offset = distance.astype(sub_phase.dtype)[None, :] + sub_phase[:, None]
    weight = jnp.sinc(offset) * jnp.sinc(offset / 3.0)
    return jnp.where(jnp.abs(offset) < 3.0, weight, jnp.zeros_like(weight))


def lanczos_batch(band_shift, sub_phase, side_len):
    positions = jnp.arange(side_len, dtype=jnp.int32)
    whole = positions[None, :, None] + band_shift[:, None, None] - positions[None, None, :]
    weights = tap_weights(sub_phase)
    matrix = jnp.zeros(whole.shape, sub_phase.dtype)
    for tap in range(TAPS):
        matrix = jnp.where(whole == tap - 3, weights[:, tap][:, None, None], matrix)
    return matrix


def warp_batch(slab_images, row_shift, col_shift, row_phase, col_phase):
    side_len = slab_images.shape[1]
    left_matrix = lanczos_batch(row_shift, row_phase, side_len)
    middle = jnp.einsum("kia,kab->kib", left_matrix, slab_images, precision=warp_mode)
    right_matrix = lanczos_batch(col_shift, col_phase, side_len)
    return jnp.einsum("kib,kjb->kij", middle, right_matrix, precision=warp_mode)


def chebyshev_rows(first_pixel, side_len):
    pixels = (first_pixel + jnp.arange(side_len, dtype=jnp.int32)).astype(jnp.float32)
    coordinate = (2.0 * pixels + 1.0) / TILE - 1.0
    orders = jnp.arange(TERMS, dtype=jnp.int32).astype(jnp.float32)
    return jnp.cos(orders[:, None] * jnp.arccos(coordinate)[None, :])


def basis_pair(anchor_pairs, side_len):
    row_basis = jax.vmap(lambda first_pixel: chebyshev_rows(first_pixel, side_len))(
        anchor_pairs[:, 0]
    )
    col_basis = jax.vmap(lambda first_pixel: chebyshev_rows(first_pixel, side_len))(
        anchor_pairs[:, 1]
    )
    return (row_basis, col_basis)


def project_terms(differences, row_basis, col_basis):
    middle = jnp.einsum("mtp,mpq->mtq", row_basis, differences, precision=exact_mode)
    return jnp.einsum("mtq,muq->mtu", middle, col_basis, precision=exact_mode)


def ring_sum(value, axis_name):
    count = lax.axis_size(axis_name)
    me = lax.axis_index(axis_name)
    received = [value]
    for step in range(1, count):
        pairs = [(i, (i + step) % count) for i in range(count)]
        received.append(lax.ppermute(value, axis_name, pairs))
    stacked = jnp.stack(received)
    total = None
    for source in range(count):
        term = lax.dynamic_index_in_dim(stacked, (me - source) % count, 0, keepdims=False)
        total = term if total is None else total + term
    return total


def body(pieces, ref_patch, piece_patch, piece_visit, anchors, shifts, phases):
    piece_count = pieces.shape[0]
    side_len = pieces.shape[1]
    patch_count = lax.axis_size(PATCH_PARTS)
    y_count = lax.axis_size("vy")
    core_count = lax.axis_size("vc")
    slab_rows = ref_patch.shape[1]
    half = lax.all_gather(ref_patch, PATCH_PARTS + ("vy",), axis=0, tiled=True)
    other = lax.ppermute(half, "vc", [(0, 1), (1, 0)])
    half = half.reshape(patch_count, y_count, slab_rows, side_len)
    other = other.reshape(patch_count, y_count, slab_rows, side_len)
    core = lax.axis_index("vc")

    warped_all = warp_batch(pieces, shifts[:, 0], shifts[:, 1], phases[:, 0], phases[:, 1])
    warped_all = lax.optimization_barrier(warped_all)

    own_rows = jnp.take(half, piece_patch, axis=0)
    other_rows = jnp.take(other, piece_patch, axis=0)
    first = jnp.where(core == 0, own_rows, other_rows)
    second = jnp.where(core == 0, other_rows, own_rows)
    ref_rows = jnp.stack([first, second], axis=2).reshape(piece_count, side_len, side_len)
    own_diffs = warped_all - ref_rows

    row_basis, col_basis = basis_pair(anchors, side_len)
    partial_value = project_terms(own_diffs, row_basis, col_basis)
    visit_slots = jnp.arange(VIS_DEV, dtype=jnp.int32)
    own_onehot = (piece_visit[:, None] == visit_slots[None, :]).astype(jnp.float32)
    local_sums = jnp.einsum("kv,ktu->vtu", own_onehot, partial_value, precision=exact_mode)
    totals = ring_sum(ring_sum(local_sums, "pz"), "px")
    coefficients = totals / float(patch_count * (piece_count // VIS_DEV) * side_len * side_len)
    chosen = jnp.take(coefficients, piece_visit, axis=0)
    middle = jnp.einsum("ktp,ktu->kpu", row_basis, chosen, precision=warp_mode)
    fitted = jnp.einsum("kpu,kuq->kpq", middle, col_basis, precision=warp_mode)
    return (own_diffs - fitted, coefficients)


def solution(mesh):
    visit_size = mesh.shape["visit"]
    patch_size = mesh.shape["patch"]
    fine = Mesh(
        mesh.devices.reshape(visit_size // 2, 2, 4, patch_size // 4),
        PIECE_AXES,
    )
    return jax.shard_map(
        body,
        mesh=fine,
        in_specs=(
            P(PIECE_AXES, None, None),
            P(PATCH_PARTS, VISIT_PARTS, None),
            P(PIECE_AXES),
            P(PIECE_AXES),
            P(PIECE_AXES, None),
            P(PIECE_AXES, None),
            P(PIECE_AXES, None),
        ),
        out_specs=(P(PIECE_AXES, None, None), P(VISIT_PARTS, None, None)),
        check_vma=False,
    )
```

```python
import jax
import jax.numpy as jnp
from jax import lax
from jax.sharding import Mesh
from jax.sharding import PartitionSpec as P

VIS_DEV = 4
TERMS = 17
TILE = 4096
TAPS = 6
CAP = 2

VISIT_PARTS = ("vy", "vc")
PATCH_PARTS = ("px", "pz")
PIECE_AXES = VISIT_PARTS + PATCH_PARTS

exact_mode = lax.Precision.HIGHEST
warp_mode = lax.Precision.HIGH


def tap_weights(sub_phase):
    distance = jnp.arange(-3, 3, dtype=jnp.int32)
    offset = distance.astype(sub_phase.dtype)[None, :] + sub_phase[:, None]
    weight = jnp.sinc(offset) * jnp.sinc(offset / 3.0)
    return jnp.where(jnp.abs(offset) < 3.0, weight, jnp.zeros_like(weight))


def lanczos_batch(band_shift, sub_phase, side_len):
    positions = jnp.arange(side_len, dtype=jnp.int32)
    whole = positions[None, :, None] + band_shift[:, None, None] - positions[None, None, :]
    weights = tap_weights(sub_phase)
    matrix = jnp.zeros(whole.shape, sub_phase.dtype)
    for tap in range(TAPS):
        matrix = jnp.where(whole == tap - 3, weights[:, tap][:, None, None], matrix)
    return matrix


def warp_batch(slab_images, row_shift, col_shift, row_phase, col_phase):
    side_len = slab_images.shape[1]
    left_matrix = lanczos_batch(row_shift, row_phase, side_len)
    middle = jnp.einsum("kia,kab->kib", left_matrix, slab_images, precision=warp_mode)
    right_matrix = lanczos_batch(col_shift, col_phase, side_len)
    return jnp.einsum("kib,kjb->kij", middle, right_matrix, precision=warp_mode)


def chebyshev_rows(first_pixel, side_len):
    pixels = (first_pixel + jnp.arange(side_len, dtype=jnp.int32)).astype(jnp.float32)
    coordinate = (2.0 * pixels + 1.0) / TILE - 1.0
    orders = jnp.arange(TERMS, dtype=jnp.int32).astype(jnp.float32)
    return jnp.cos(orders[:, None] * jnp.arccos(coordinate)[None, :])


def basis_batch(first_pixels, side_len):
    return jax.vmap(lambda first_pixel: chebyshev_rows(first_pixel, side_len))(first_pixels)


def ring_gather(value, axis_name):
    count = lax.axis_size(axis_name)
    me = lax.axis_index(axis_name)
    received = [value]
    for step in range(1, count):
        pairs = [(i, (i + step) % count) for i in range(count)]
        received.append(lax.ppermute(value, axis_name, pairs))
    stacked = jnp.stack(received)
    order = (me - jnp.arange(count, dtype=jnp.int32)) % count
    return jnp.take(stacked, order, axis=0)


def ring_sum(value, axis_name):
    stacked = ring_gather(value, axis_name)
    total = stacked[0]
    for source in range(1, stacked.shape[0]):
        total = total + stacked[source]
    return total


def body(pieces, ref_patch, piece_patch, piece_visit, anchors, shifts, phases):
    piece_count = pieces.shape[0]
    side_len = pieces.shape[1]
    slab_rows = ref_patch.shape[1]
    patch_count = lax.axis_size(PATCH_PARTS)
    visit_count = lax.axis_size(VISIT_PARTS)
    device_count = patch_count * visit_count
    total_visits = visit_count * VIS_DEV
    my_visit_row = lax.axis_index(VISIT_PARTS)
    my_patch = lax.axis_index(PATCH_PARTS)

    gathered = lax.all_gather(ref_patch, PATCH_PARTS + VISIT_PARTS, axis=0, tiled=True)
    ref_block = gathered.reshape(patch_count, side_len, side_len)

    global_visit = my_visit_row * VIS_DEV + piece_visit
    visit_ids = jnp.arange(total_visits, dtype=jnp.int32)

    warped_all = warp_batch(pieces, shifts[:, 0], shifts[:, 1], phases[:, 0], phases[:, 1])
    warped_all = lax.optimization_barrier(warped_all)
    row_basis = basis_batch(anchors[:, 0], side_len)
    col_basis = basis_batch(anchors[:, 1], side_len)
    middle = jnp.einsum("mtp,mpq->mtq", row_basis, warped_all, precision=exact_mode)
    warp_terms = jnp.einsum("mtq,muq->mtu", middle, col_basis, precision=exact_mode)
    own_onehot = (global_visit[:, None] == visit_ids[None, :]).astype(jnp.float32)
    warp_sums = jnp.einsum("kv,ktu->vtu", own_onehot, warp_terms, precision=exact_mode)

    meta = jnp.stack([piece_patch, global_visit, anchors[:, 0], anchors[:, 1]], axis=1)
    for axis_name in ("pz", "px", "vc", "vy"):
        meta = ring_gather(meta, axis_name)
    meta = meta.reshape(device_count * piece_count, 4)
    on_mine = meta[:, 0] == my_patch
    slots = CAP * device_count
    (chosen_pieces,) = jnp.nonzero(on_mine, size=slots, fill_value=0)
    valid = (jnp.arange(slots) < jnp.sum(on_mine.astype(jnp.int32))).astype(jnp.float32)
    chosen_meta = jnp.take(meta, chosen_pieces, axis=0)
    slab_row_basis = basis_batch(chosen_meta[:, 2] + my_visit_row * slab_rows, slab_rows)
    slab_col_basis = basis_batch(chosen_meta[:, 3], side_len)
    slab_middle = jnp.einsum("stp,pq->stq", slab_row_basis, ref_patch[0], precision=exact_mode)
    slab_terms = jnp.einsum("stq,suq->stu", slab_middle, slab_col_basis, precision=exact_mode)
    slab_onehot = (chosen_meta[:, 1][:, None] == visit_ids[None, :]).astype(jnp.float32)
    slab_onehot = slab_onehot * valid[:, None]
    slab_sums = jnp.einsum("sv,stu->vtu", slab_onehot, slab_terms, precision=exact_mode)

    totals = warp_sums - slab_sums
    for axis_name in ("pz", "px", "vc", "vy"):
        totals = ring_sum(totals, axis_name)
    all_coefficients = totals / float(patch_count * (piece_count // VIS_DEV) * side_len * side_len)
    coefficients = lax.dynamic_slice_in_dim(all_coefficients, my_visit_row * VIS_DEV, VIS_DEV, 0)

    chosen = jnp.take(all_coefficients, global_visit, axis=0)
    fit_middle = jnp.einsum("ktp,ktu->kpu", row_basis, chosen, precision=warp_mode)
    fitted = jnp.einsum("kpu,kuq->kpq", fit_middle, col_basis, precision=warp_mode)
    own_diffs = warped_all - jnp.take(ref_block, piece_patch, axis=0)
    return (own_diffs - fitted, coefficients)


def solution(mesh):
    visit_size = mesh.shape["visit"]
    patch_size = mesh.shape["patch"]
    fine = Mesh(
        mesh.devices.reshape(visit_size // 2, 2, 4, patch_size // 4),
        PIECE_AXES,
    )
    return jax.shard_map(
        body,
        mesh=fine,
        in_specs=(
            P(PIECE_AXES, None, None),
            P(PATCH_PARTS, VISIT_PARTS, None),
            P(PIECE_AXES),
            P(PIECE_AXES),
            P(PIECE_AXES, None),
            P(PIECE_AXES, None),
            P(PIECE_AXES, None),
        ),
        out_specs=(P(PIECE_AXES, None, None), P(VISIT_PARTS, None, None)),
        check_vma=False,
    )
```

```python
import jax
import jax.numpy as jnp
from jax import lax
from jax.sharding import Mesh
from jax.sharding import PartitionSpec as P

VIS_DEV = 4
TERMS = 17
TILE = 4096
TAPS = 6
CAP = 2

VISIT_PARTS = ("vy", "vc")
PATCH_PARTS = ("px", "pz")
PIECE_AXES = VISIT_PARTS + PATCH_PARTS

exact_mode = lax.Precision.HIGHEST
warp_mode = lax.Precision.HIGH


def tap_weights(sub_phase):
    distance = jnp.arange(-3, 3, dtype=jnp.int32)
    offset = distance.astype(sub_phase.dtype)[None, :] + sub_phase[:, None]
    weight = jnp.sinc(offset) * jnp.sinc(offset / 3.0)
    return jnp.where(jnp.abs(offset) < 3.0, weight, jnp.zeros_like(weight))


def lanczos_batch(band_shift, sub_phase, side_len):
    positions = jnp.arange(side_len, dtype=jnp.int32)
    whole = positions[None, :, None] + band_shift[:, None, None] - positions[None, None, :]
    weights = tap_weights(sub_phase)
    matrix = jnp.zeros(whole.shape, sub_phase.dtype)
    for tap in range(TAPS):
        matrix = jnp.where(whole == tap - 3, weights[:, tap][:, None, None], matrix)
    return matrix


def warp_batch(slab_images, row_shift, col_shift, row_phase, col_phase):
    side_len = slab_images.shape[1]
    left_matrix = lanczos_batch(row_shift, row_phase, side_len)
    middle = jnp.einsum("kia,kab->kib", left_matrix, slab_images, precision=warp_mode)
    right_matrix = lanczos_batch(col_shift, col_phase, side_len)
    return jnp.einsum("kib,kjb->kij", middle, right_matrix, precision=warp_mode)


def chebyshev_rows(first_pixel, side_len):
    pixels = (first_pixel + jnp.arange(side_len, dtype=jnp.int32)).astype(jnp.float32)
    coordinate = (2.0 * pixels + 1.0) / TILE - 1.0
    orders = jnp.arange(TERMS, dtype=jnp.int32).astype(jnp.float32)
    return jnp.cos(orders[:, None] * jnp.arccos(coordinate)[None, :])


def basis_batch(first_pixels, side_len):
    return jax.vmap(lambda first_pixel: chebyshev_rows(first_pixel, side_len))(first_pixels)


def ring_gather(value, axis_name):
    count = lax.axis_size(axis_name)
    me = lax.axis_index(axis_name)
    received = [value]
    for step in range(1, count):
        pairs = [(i, (i + step) % count) for i in range(count)]
        received.append(lax.ppermute(value, axis_name, pairs))
    stacked = jnp.stack(received)
    order = (me - jnp.arange(count, dtype=jnp.int32)) % count
    return jnp.take(stacked, order, axis=0)


def ring_sum(value, axis_name):
    stacked = ring_gather(value, axis_name)
    total = stacked[0]
    for source in range(1, stacked.shape[0]):
        total = total + stacked[source]
    return total


def body(pieces, ref_patch, piece_patch, piece_visit, anchors, shifts, phases):
    piece_count = pieces.shape[0]
    side_len = pieces.shape[1]
    slab_rows = ref_patch.shape[1]
    patch_count = lax.axis_size(PATCH_PARTS)
    visit_count = lax.axis_size(VISIT_PARTS)
    device_count = patch_count * visit_count
    total_visits = visit_count * VIS_DEV
    my_visit_row = lax.axis_index(VISIT_PARTS)
    my_patch = lax.axis_index(PATCH_PARTS)

    gathered = lax.all_gather(ref_patch, PATCH_PARTS + VISIT_PARTS, axis=0, tiled=True)
    ref_block = gathered.reshape(patch_count, side_len, side_len)

    global_visit = my_visit_row * VIS_DEV + piece_visit
    visit_ids = jnp.arange(total_visits, dtype=jnp.int32)

    warped_all = warp_batch(pieces, shifts[:, 0], shifts[:, 1], phases[:, 0], phases[:, 1])
    warped_all = lax.optimization_barrier(warped_all)
    row_basis = basis_batch(anchors[:, 0], side_len)
    col_basis = basis_batch(anchors[:, 1], side_len)
    middle = jnp.einsum("mtp,mpq->mtq", row_basis, warped_all, precision=exact_mode)
    warp_terms = jnp.einsum("mtq,muq->mtu", middle, col_basis, precision=exact_mode)
    own_onehot = (global_visit[:, None] == visit_ids[None, :]).astype(jnp.float32)
    warp_sums = jnp.einsum("kv,ktu->vtu", own_onehot, warp_terms, precision=exact_mode)

    meta = jnp.stack([piece_patch, global_visit, anchors[:, 0], anchors[:, 1]], axis=1)
    meta = ring_gather(ring_gather(meta, PATCH_PARTS), VISIT_PARTS)
    meta = meta.reshape(device_count, piece_count, 4)
    on_mine = meta[:, :, 0] == my_patch
    slot_meta = []
    slot_valid = []
    remaining = on_mine
    for _ in range(CAP):
        pick = jnp.argmax(remaining, axis=1)
        slot_valid.append(jnp.take_along_axis(remaining, pick[:, None], axis=1)[:, 0])
        slot_meta.append(jnp.take_along_axis(meta, pick[:, None, None], axis=1)[:, 0, :])
        remaining = remaining & (jnp.arange(piece_count)[None, :] != pick[:, None])
    chosen_meta = jnp.concatenate(slot_meta, axis=0)
    valid = jnp.concatenate(slot_valid, axis=0).astype(jnp.float32)
    slab_row_basis = basis_batch(chosen_meta[:, 2] + my_visit_row * slab_rows, slab_rows)
    slab_col_basis = basis_batch(chosen_meta[:, 3], side_len)
    slots = slab_col_basis.shape[0]
    against_cols = jnp.einsum(
        "pq,xq->px", ref_patch[0], slab_col_basis.reshape(slots * TERMS, side_len), precision=exact_mode
    ).reshape(slab_rows, slots, TERMS)
    slab_terms = jnp.sum(
        slab_row_basis[:, :, :, None] * jnp.transpose(against_cols, (1, 0, 2))[:, None, :, :], axis=2
    )
    slab_onehot = (chosen_meta[:, 1][:, None] == visit_ids[None, :]).astype(jnp.float32)
    slab_onehot = slab_onehot * valid[:, None]
    slab_sums = jnp.einsum("sv,stu->vtu", slab_onehot, slab_terms, precision=exact_mode)

    totals = warp_sums - slab_sums
    totals = ring_sum(ring_sum(totals, PATCH_PARTS), VISIT_PARTS)
    all_coefficients = totals / float(patch_count * (piece_count // VIS_DEV) * side_len * side_len)
    coefficients = lax.dynamic_slice_in_dim(all_coefficients, my_visit_row * VIS_DEV, VIS_DEV, 0)

    chosen = jnp.take(all_coefficients, global_visit, axis=0)
    fit_middle = jnp.einsum("ktp,ktu->kpu", row_basis, chosen, precision=warp_mode)
    fitted = jnp.einsum("kpu,kuq->kpq", fit_middle, col_basis, precision=warp_mode)
    own_diffs = warped_all - jnp.take(ref_block, piece_patch, axis=0)
    return (own_diffs - fitted, coefficients)


def solution(mesh):
    visit_size = mesh.shape["visit"]
    patch_size = mesh.shape["patch"]
    fine = Mesh(
        mesh.devices.reshape(visit_size // 2, 2, 4, patch_size // 4),
        PIECE_AXES,
    )
    return jax.shard_map(
        body,
        mesh=fine,
        in_specs=(
            P(PIECE_AXES, None, None),
            P(PATCH_PARTS, VISIT_PARTS, None),
            P(PIECE_AXES),
            P(PIECE_AXES),
            P(PIECE_AXES, None),
            P(PIECE_AXES, None),
            P(PIECE_AXES, None),
        ),
        out_specs=(P(PIECE_AXES, None, None), P(VISIT_PARTS, None, None)),
        check_vma=False,
    )
```

```python
import jax
import jax.numpy as jnp
from jax import lax
from jax.sharding import PartitionSpec as P

VIS_DEV = 4
TERMS = 17
TILE = 4096
TAPS = 6


exact_mode = lax.Precision.HIGHEST
warp_mode = lax.Precision.HIGH


def tap_weights(sub_phase):
    distance = jnp.arange(-3, 3, dtype=jnp.int32)
    offset = distance.astype(sub_phase.dtype)[None, :] + sub_phase[:, None]
    weight = jnp.sinc(offset) * jnp.sinc(offset / 3.0)
    return jnp.where(jnp.abs(offset) < 3.0, weight, jnp.zeros_like(weight))


def lanczos_batch(band_shift, sub_phase, side_len):
    positions = jnp.arange(side_len, dtype=jnp.int32)
    whole = positions[None, :, None] + band_shift[:, None, None] - positions[None, None, :]
    weights = tap_weights(sub_phase)
    matrix = jnp.zeros(whole.shape, sub_phase.dtype)
    for tap in range(TAPS):
        matrix = jnp.where(whole == tap - 3, weights[:, tap][:, None, None], matrix)
    return matrix


def warp_batch(slab_images, row_shift, col_shift, row_phase, col_phase):
    side_len = slab_images.shape[1]
    left_matrix = lanczos_batch(row_shift, row_phase, side_len)
    middle = jnp.einsum("kia,kab->kib", left_matrix, slab_images, precision=warp_mode)
    right_matrix = lanczos_batch(col_shift, col_phase, side_len)
    return jnp.einsum("kib,kjb->kij", middle, right_matrix, precision=warp_mode)


def chebyshev_rows(first_pixel, side_len):
    pixels = (first_pixel + jnp.arange(side_len, dtype=jnp.int32)).astype(jnp.float32)
    coordinate = (2.0 * pixels + 1.0) / TILE - 1.0
    orders = jnp.arange(TERMS, dtype=jnp.int32).astype(jnp.float32)
    return jnp.cos(orders[:, None] * jnp.arccos(coordinate)[None, :])


def basis_pair(anchor_pairs, side_len):
    row_basis = jax.vmap(lambda first_pixel: chebyshev_rows(first_pixel, side_len))(
        anchor_pairs[:, 0]
    )
    col_basis = jax.vmap(lambda first_pixel: chebyshev_rows(first_pixel, side_len))(
        anchor_pairs[:, 1]
    )
    return (row_basis, col_basis)


def project_terms(differences, row_basis, col_basis):
    middle = jnp.einsum("mtp,mpq->mtq", row_basis, differences, precision=exact_mode)
    return jnp.einsum("mtq,muq->mtu", middle, col_basis, precision=exact_mode)


def butterfly_sum(value, axis_name):
    count = lax.axis_size(axis_name)
    stride = 1
    while stride < count:
        pairs = [(i, i ^ stride) for i in range(count)]
        value = value + lax.ppermute(value, axis_name, pairs)
        stride *= 2
    return value


def body(pieces, ref_patch, piece_patch, piece_visit, anchors, shifts, phases):
    piece_count = pieces.shape[0]
    side_len = pieces.shape[1]
    patch_count = lax.axis_size("patch")
    gathered = lax.all_gather(ref_patch, ("patch", "visit"), axis=0, tiled=True)
    ref_block = gathered.reshape(patch_count, side_len, side_len)
    visit_slots = jnp.arange(VIS_DEV, dtype=jnp.int32)
    own_onehot = (piece_visit[:, None] == visit_slots[None, :]).astype(jnp.float32)
    warped_all = warp_batch(pieces, shifts[:, 0], shifts[:, 1], phases[:, 0], phases[:, 1])
    warped_all = lax.optimization_barrier(warped_all)
    own_diffs = warped_all - jnp.take(ref_block, piece_patch, axis=0)
    row_basis, col_basis = basis_pair(anchors, side_len)
    partial_value = project_terms(own_diffs, row_basis, col_basis)
    local_sums = jnp.einsum("kv,ktu->vtu", own_onehot, partial_value, precision=exact_mode)
    totals = butterfly_sum(local_sums, "patch")
    coefficients = totals / float(patch_count * (piece_count // VIS_DEV) * side_len * side_len)
    chosen = jnp.take(coefficients, piece_visit, axis=0)
    middle = jnp.einsum("ktp,ktu->kpu", row_basis, chosen, precision=warp_mode)
    fitted = jnp.einsum("kpu,kuq->kpq", middle, col_basis, precision=warp_mode)
    return (own_diffs - fitted, coefficients)


def solution(mesh):
    return jax.shard_map(
        body,
        mesh=mesh,
        in_specs=(
            P(("visit", "patch"), None, None),
            P("patch", "visit", None),
            P(("visit", "patch")),
            P(("visit", "patch")),
            P(("visit", "patch"), None),
            P(("visit", "patch"), None),
            P(("visit", "patch"), None),
        ),
        out_specs=(P(("visit", "patch"), None, None), P("visit", None, None)),
        check_vma=False,
    )
```

```python
import jax
import jax.numpy as jnp
from jax import lax
from jax.sharding import Mesh
from jax.sharding import PartitionSpec as P

VIS_DEV = 4
TERMS = 17
TILE = 4096
TAPS = 6
CAP = 2

VISIT_PARTS = ("vy", "vc")
PATCH_PARTS = ("px", "pz")
PIECE_AXES = VISIT_PARTS + PATCH_PARTS

exact_mode = lax.Precision.HIGHEST
warp_mode = lax.Precision.HIGH


def tap_weights(sub_phase):
    distance = jnp.arange(-3, 3, dtype=jnp.int32)
    offset = distance.astype(sub_phase.dtype)[None, :] + sub_phase[:, None]
    weight = jnp.sinc(offset) * jnp.sinc(offset / 3.0)
    return jnp.where(jnp.abs(offset) < 3.0, weight, jnp.zeros_like(weight))


def lanczos_batch(band_shift, sub_phase, side_len):
    positions = jnp.arange(side_len, dtype=jnp.int32)
    whole = positions[None, :, None] + band_shift[:, None, None] - positions[None, None, :]
    weights = tap_weights(sub_phase)
    matrix = jnp.zeros(whole.shape, sub_phase.dtype)
    for tap in range(TAPS):
        matrix = jnp.where(whole == tap - 3, weights[:, tap][:, None, None], matrix)
    return matrix


def warp_batch(slab_images, row_shift, col_shift, row_phase, col_phase):
    side_len = slab_images.shape[1]
    left_matrix = lanczos_batch(row_shift, row_phase, side_len)
    middle = jnp.einsum("kia,kab->kib", left_matrix, slab_images, precision=warp_mode)
    right_matrix = lanczos_batch(col_shift, col_phase, side_len)
    return jnp.einsum("kib,kjb->kij", middle, right_matrix, precision=warp_mode)


def chebyshev_rows(first_pixel, side_len):
    pixels = (first_pixel + jnp.arange(side_len, dtype=jnp.int32)).astype(jnp.float32)
    coordinate = (2.0 * pixels + 1.0) / TILE - 1.0
    orders = jnp.arange(TERMS, dtype=jnp.int32).astype(jnp.float32)
    return jnp.cos(orders[:, None] * jnp.arccos(coordinate)[None, :])


def recurrence_batch(first_pixels, side_len):
    pixels = (first_pixels[:, None] + jnp.arange(side_len, dtype=jnp.int32)[None, :]).astype(jnp.float32)
    coordinate = (2.0 * pixels + 1.0) / TILE - 1.0
    terms = [jnp.ones_like(coordinate), coordinate]
    for _ in range(2, TERMS):
        terms.append(2.0 * coordinate * terms[-1] - terms[-2])
    return jnp.stack(terms, axis=1)


def butterfly_sum(value, axis_names):
    count = lax.axis_size(axis_names)
    stride = 1
    while stride < count:
        pairs = [(i, i ^ stride) for i in range(count)]
        value = value + lax.ppermute(value, axis_names, pairs)
        stride *= 2
    return value


def basis_batch(first_pixels, side_len):
    return jax.vmap(lambda first_pixel: chebyshev_rows(first_pixel, side_len))(first_pixels)


def ring_gather(value, axis_name):
    count = lax.axis_size(axis_name)
    me = lax.axis_index(axis_name)
    received = [value]
    for step in range(1, count):
        pairs = [(i, (i + step) % count) for i in range(count)]
        received.append(lax.ppermute(value, axis_name, pairs))
    stacked = jnp.stack(received)
    order = (me - jnp.arange(count, dtype=jnp.int32)) % count
    return jnp.take(stacked, order, axis=0)


def ring_sum(value, axis_name):
    stacked = ring_gather(value, axis_name)
    total = stacked[0]
    for source in range(1, stacked.shape[0]):
        total = total + stacked[source]
    return total


def body(pieces, ref_patch, piece_patch, piece_visit, anchors, shifts, phases):
    piece_count = pieces.shape[0]
    side_len = pieces.shape[1]
    slab_rows = ref_patch.shape[1]
    patch_count = lax.axis_size(PATCH_PARTS)
    visit_count = lax.axis_size(VISIT_PARTS)
    device_count = patch_count * visit_count
    total_visits = visit_count * VIS_DEV
    my_visit_row = lax.axis_index(VISIT_PARTS)
    my_patch = lax.axis_index(PATCH_PARTS)

    global_visit = my_visit_row * VIS_DEV + piece_visit
    visit_ids = jnp.arange(total_visits, dtype=jnp.int32)

    meta = jnp.stack([piece_patch, global_visit, anchors[:, 0], anchors[:, 1]], axis=1)
    meta = lax.all_gather(meta, PIECE_AXES, axis=0, tiled=True)
    meta, ref_in = lax.optimization_barrier((meta, ref_patch))
    gathered = lax.all_gather(ref_in, PATCH_PARTS + VISIT_PARTS, axis=0, tiled=True)
    ref_block = gathered.reshape(patch_count, side_len, side_len)

    warped_all = warp_batch(pieces, shifts[:, 0], shifts[:, 1], phases[:, 0], phases[:, 1])
    warped_all = lax.optimization_barrier(warped_all)
    row_basis = basis_batch(anchors[:, 0], side_len)
    col_basis = basis_batch(anchors[:, 1], side_len)
    middle = jnp.einsum("mtp,mpq->mtq", row_basis, warped_all, precision=exact_mode)
    warp_terms = jnp.einsum("mtq,muq->mtu", middle, col_basis, precision=exact_mode)
    own_onehot = (global_visit[:, None] == visit_ids[None, :]).astype(jnp.float32)
    warp_sums = jnp.einsum("kv,ktu->vtu", own_onehot, warp_terms, precision=exact_mode)

    meta = meta.reshape(device_count, piece_count, 4)
    on_mine = meta[:, :, 0] == my_patch
    slot_meta = []
    slot_valid = []
    remaining = on_mine
    for _ in range(CAP):
        pick = jnp.argmax(remaining, axis=1)
        slot_valid.append(jnp.take_along_axis(remaining, pick[:, None], axis=1)[:, 0])
        slot_meta.append(jnp.take_along_axis(meta, pick[:, None, None], axis=1)[:, 0, :])
        remaining = remaining & (jnp.arange(piece_count)[None, :] != pick[:, None])
    chosen_meta = jnp.concatenate(slot_meta, axis=0)
    valid = jnp.concatenate(slot_valid, axis=0).astype(jnp.float32)
    slab_row_basis = recurrence_batch(chosen_meta[:, 2] + my_visit_row * slab_rows, slab_rows)
    slab_col_basis = recurrence_batch(chosen_meta[:, 3], side_len)
    slots = slab_col_basis.shape[0]
    against_cols = jnp.einsum(
        "pq,xq->px", ref_patch[0], slab_col_basis.reshape(slots * TERMS, side_len), precision=exact_mode
    ).reshape(slab_rows, slots, TERMS)
    slab_terms = jnp.einsum("stp,psu->stu", slab_row_basis, against_cols, precision=exact_mode)
    slab_onehot = (chosen_meta[:, 1][:, None] == visit_ids[None, :]).astype(jnp.float32)
    slab_onehot = slab_onehot * valid[:, None]
    slab_sums = jnp.einsum("sv,stu->vtu", slab_onehot, slab_terms, precision=exact_mode)

    totals = butterfly_sum(warp_sums - slab_sums, PIECE_AXES)
    all_coefficients = totals / float(patch_count * (piece_count // VIS_DEV) * side_len * side_len)
    coefficients = lax.dynamic_slice_in_dim(all_coefficients, my_visit_row * VIS_DEV, VIS_DEV, 0)

    chosen = jnp.take(all_coefficients, global_visit, axis=0)
    fit_middle = jnp.einsum("ktp,ktu->kpu", row_basis, chosen, precision=warp_mode)
    fitted = jnp.einsum("kpu,kuq->kpq", fit_middle, col_basis, precision=warp_mode)
    own_diffs = warped_all - jnp.take(ref_block, piece_patch, axis=0)
    return (own_diffs - fitted, coefficients)


def solution(mesh):
    visit_size = mesh.shape["visit"]
    patch_size = mesh.shape["patch"]
    fine = Mesh(
        mesh.devices.reshape(visit_size // 2, 2, 4, patch_size // 4),
        PIECE_AXES,
    )
    return jax.shard_map(
        body,
        mesh=fine,
        in_specs=(
            P(PIECE_AXES, None, None),
            P(PATCH_PARTS, VISIT_PARTS, None),
            P(PIECE_AXES),
            P(PIECE_AXES),
            P(PIECE_AXES, None),
            P(PIECE_AXES, None),
            P(PIECE_AXES, None),
        ),
        out_specs=(P(PIECE_AXES, None, None), P(VISIT_PARTS, None, None)),
        check_vma=False,
    )
```

```python
import jax
import jax.numpy as jnp
from jax import lax
from jax.sharding import PartitionSpec as P

VIS_DEV = 4
TERMS = 17
TILE = 4096
TAPS = 6


exact_mode = lax.Precision.HIGHEST
warp_mode = lax.Precision.HIGH


def tap_weights(sub_phase):
    distance = jnp.arange(-3, 3, dtype=jnp.int32)
    offset = distance.astype(sub_phase.dtype)[None, :] + sub_phase[:, None]
    weight = jnp.sinc(offset) * jnp.sinc(offset / 3.0)
    return jnp.where(jnp.abs(offset) < 3.0, weight, jnp.zeros_like(weight))


def lanczos_batch(band_shift, sub_phase, side_len):
    positions = jnp.arange(side_len, dtype=jnp.int32)
    whole = positions[None, :, None] + band_shift[:, None, None] - positions[None, None, :]
    weights = tap_weights(sub_phase)
    matrix = jnp.zeros(whole.shape, sub_phase.dtype)
    for tap in range(TAPS):
        matrix = jnp.where(whole == tap - 3, weights[:, tap][:, None, None], matrix)
    return matrix


def warp_batch(slab_images, row_shift, col_shift, row_phase, col_phase):
    side_len = slab_images.shape[1]
    left_matrix = lanczos_batch(row_shift, row_phase, side_len)
    middle = jnp.einsum("kia,kab->kib", left_matrix, slab_images, precision=warp_mode)
    right_matrix = lanczos_batch(col_shift, col_phase, side_len)
    return jnp.einsum("kib,kjb->kij", middle, right_matrix, precision=warp_mode)


def chebyshev_rows(first_pixel, side_len):
    pixels = (first_pixel + jnp.arange(side_len, dtype=jnp.int32)).astype(jnp.float32)
    coordinate = (2.0 * pixels + 1.0) / TILE - 1.0
    orders = jnp.arange(TERMS, dtype=jnp.int32).astype(jnp.float32)
    return jnp.cos(orders[:, None] * jnp.arccos(coordinate)[None, :])


def basis_pair(anchor_pairs, side_len):
    row_basis = jax.vmap(lambda first_pixel: chebyshev_rows(first_pixel, side_len))(
        anchor_pairs[:, 0]
    )
    col_basis = jax.vmap(lambda first_pixel: chebyshev_rows(first_pixel, side_len))(
        anchor_pairs[:, 1]
    )
    return (row_basis, col_basis)


def project_terms(differences, row_basis, col_basis):
    middle = jnp.einsum("mtp,mpq->mtq", row_basis, differences, precision=warp_mode)
    return jnp.einsum("mtq,muq->mtu", middle, col_basis, precision=exact_mode)


def butterfly_sum(value, axis_name):
    count = lax.axis_size(axis_name)
    stride = 1
    while stride < count:
        pairs = [(i, i ^ stride) for i in range(count)]
        value = value + lax.ppermute(value, axis_name, pairs)
        stride *= 2
    return value


def body(pieces, ref_patch, piece_patch, piece_visit, anchors, shifts, phases):
    piece_count = pieces.shape[0]
    side_len = pieces.shape[1]
    patch_count = lax.axis_size("patch")
    gathered = lax.all_gather(ref_patch, ("patch", "visit"), axis=0, tiled=True)
    ref_block = gathered.reshape(patch_count, side_len, side_len)
    visit_slots = jnp.arange(VIS_DEV, dtype=jnp.int32)
    own_onehot = (piece_visit[:, None] == visit_slots[None, :]).astype(jnp.float32)
    warped_all = warp_batch(pieces, shifts[:, 0], shifts[:, 1], phases[:, 0], phases[:, 1])
    warped_all = lax.optimization_barrier(warped_all)
    own_diffs = warped_all - jnp.take(ref_block, piece_patch, axis=0)
    own_diffs = lax.optimization_barrier(own_diffs)
    row_basis, col_basis = basis_pair(anchors, side_len)
    partial_value = project_terms(own_diffs, row_basis, col_basis)
    local_sums = jnp.einsum("kv,ktu->vtu", own_onehot, partial_value, precision=exact_mode)
    totals = butterfly_sum(local_sums, "patch")
    coefficients = totals / float(patch_count * (piece_count // VIS_DEV) * side_len * side_len)
    chosen = jnp.take(coefficients, piece_visit, axis=0)
    middle = jnp.einsum("ktp,ktu->kpu", row_basis, chosen, precision=warp_mode)
    fitted = jnp.einsum("kpu,kuq->kpq", middle, col_basis, precision=warp_mode)
    return (own_diffs - fitted, coefficients)


def solution(mesh):
    return jax.shard_map(
        body,
        mesh=mesh,
        in_specs=(
            P(("visit", "patch"), None, None),
            P("patch", "visit", None),
            P(("visit", "patch")),
            P(("visit", "patch")),
            P(("visit", "patch"), None),
            P(("visit", "patch"), None),
            P(("visit", "patch"), None),
        ),
        out_specs=(P(("visit", "patch"), None, None), P("visit", None, None)),
        check_vma=False,
    )
```

```python
import jax
import jax.numpy as jnp
from jax import lax
from jax.sharding import Mesh
from jax.sharding import PartitionSpec as P

VIS_DEV = 4
TERMS = 17
TILE = 4096
TAPS = 6

VISIT_PARTS = ("vy", "vc")
PATCH_PARTS = ("px", "pz")
PIECE_AXES = VISIT_PARTS + PATCH_PARTS


exact_mode = lax.Precision.HIGHEST
warp_mode = lax.Precision.HIGH


def tap_weights(sub_phase):
    distance = jnp.arange(-3, 3, dtype=jnp.int32)
    offset = distance.astype(sub_phase.dtype)[None, :] + sub_phase[:, None]
    weight = jnp.sinc(offset) * jnp.sinc(offset / 3.0)
    return jnp.where(jnp.abs(offset) < 3.0, weight, jnp.zeros_like(weight))


def lanczos_batch(band_shift, sub_phase, side_len):
    positions = jnp.arange(side_len, dtype=jnp.int32)
    whole = positions[None, :, None] + band_shift[:, None, None] - positions[None, None, :]
    weights = tap_weights(sub_phase)
    matrix = jnp.zeros(whole.shape, sub_phase.dtype)
    for tap in range(TAPS):
        matrix = jnp.where(whole == tap - 3, weights[:, tap][:, None, None], matrix)
    return matrix


def warp_batch(slab_images, row_shift, col_shift, row_phase, col_phase):
    side_len = slab_images.shape[1]
    left_matrix = lanczos_batch(row_shift, row_phase, side_len)
    middle = jnp.einsum("kia,kab->kib", left_matrix, slab_images, precision=warp_mode)
    right_matrix = lanczos_batch(col_shift, col_phase, side_len)
    return jnp.einsum("kib,kjb->kij", middle, right_matrix, precision=warp_mode)


def chebyshev_rows(first_pixel, side_len):
    pixels = (first_pixel + jnp.arange(side_len, dtype=jnp.int32)).astype(jnp.float32)
    coordinate = (2.0 * pixels + 1.0) / TILE - 1.0
    orders = jnp.arange(TERMS, dtype=jnp.int32).astype(jnp.float32)
    return jnp.cos(orders[:, None] * jnp.arccos(coordinate)[None, :])


def basis_pair(anchor_pairs, side_len):
    row_basis = jax.vmap(lambda first_pixel: chebyshev_rows(first_pixel, side_len))(
        anchor_pairs[:, 0]
    )
    col_basis = jax.vmap(lambda first_pixel: chebyshev_rows(first_pixel, side_len))(
        anchor_pairs[:, 1]
    )
    return (row_basis, col_basis)


def project_terms(differences, row_basis, col_basis):
    middle = jnp.einsum("mtp,mpq->mtq", row_basis, differences, precision=warp_mode)
    return jnp.einsum("mtq,muq->mtu", middle, col_basis, precision=exact_mode)


def ring_sum(value, axis_name):
    count = lax.axis_size(axis_name)
    me = lax.axis_index(axis_name)
    received = [value]
    for step in range(1, count):
        pairs = [(i, (i + step) % count) for i in range(count)]
        received.append(lax.ppermute(value, axis_name, pairs))
    stacked = jnp.stack(received)
    total = None
    for source in range(count):
        term = lax.dynamic_index_in_dim(stacked, (me - source) % count, 0, keepdims=False)
        total = term if total is None else total + term
    return total


def body(pieces, ref_patch, piece_patch, piece_visit, anchors, shifts, phases):
    piece_count = pieces.shape[0]
    side_len = pieces.shape[1]
    patch_count = lax.axis_size(PATCH_PARTS)
    gathered = lax.all_gather(ref_patch, PATCH_PARTS + VISIT_PARTS, axis=0, tiled=True)
    ref_block = gathered.reshape(patch_count, side_len, side_len)
    visit_slots = jnp.arange(VIS_DEV, dtype=jnp.int32)
    own_onehot = (piece_visit[:, None] == visit_slots[None, :]).astype(jnp.float32)
    warped_all = warp_batch(pieces, shifts[:, 0], shifts[:, 1], phases[:, 0], phases[:, 1])
    warped_all = lax.optimization_barrier(warped_all)
    own_diffs = warped_all - jnp.take(ref_block, piece_patch, axis=0)
    row_basis, col_basis = basis_pair(anchors, side_len)
    partial_value = project_terms(own_diffs, row_basis, col_basis)
    local_sums = jnp.einsum("kv,ktu->vtu", own_onehot, partial_value, precision=exact_mode)
    totals = ring_sum(ring_sum(local_sums, "pz"), "px")
    coefficients = totals / float(patch_count * (piece_count // VIS_DEV) * side_len * side_len)
    chosen = jnp.take(coefficients, piece_visit, axis=0)
    middle = jnp.einsum("ktp,ktu->kpu", row_basis, chosen, precision=warp_mode)
    fitted = jnp.einsum("kpu,kuq->kpq", middle, col_basis, precision=warp_mode)
    return (own_diffs - fitted, coefficients)


def solution(mesh):
    visit_size = mesh.shape["visit"]
    patch_size = mesh.shape["patch"]
    fine = Mesh(
        mesh.devices.reshape(visit_size // 2, 2, 4, patch_size // 4),
        PIECE_AXES,
    )
    return jax.shard_map(
        body,
        mesh=fine,
        in_specs=(
            P(PIECE_AXES, None, None),
            P(PATCH_PARTS, VISIT_PARTS, None),
            P(PIECE_AXES),
            P(PIECE_AXES),
            P(PIECE_AXES, None),
            P(PIECE_AXES, None),
            P(PIECE_AXES, None),
        ),
        out_specs=(P(PIECE_AXES, None, None), P(VISIT_PARTS, None, None)),
        check_vma=False,
    )
```

```python
import jax
import jax.numpy as jnp
from jax import lax
from jax.sharding import Mesh
from jax.sharding import PartitionSpec as P

VIS_DEV = 4
TERMS = 17
TILE = 4096
TAPS = 6

VISIT_PARTS = ("vy", "vc")
PATCH_PARTS = ("px", "pz")
PIECE_AXES = VISIT_PARTS + PATCH_PARTS


exact_mode = lax.Precision.HIGHEST
warp_mode = lax.Precision.HIGH


def tap_weights(sub_phase):
    distance = jnp.arange(-3, 3, dtype=jnp.int32)
    offset = distance.astype(sub_phase.dtype)[None, :] + sub_phase[:, None]
    weight = jnp.sinc(offset) * jnp.sinc(offset / 3.0)
    return jnp.where(jnp.abs(offset) < 3.0, weight, jnp.zeros_like(weight))


def lanczos_batch(band_shift, sub_phase, side_len):
    positions = jnp.arange(side_len, dtype=jnp.int32)
    whole = positions[None, :, None] + band_shift[:, None, None] - positions[None, None, :]
    weights = tap_weights(sub_phase)
    matrix = jnp.zeros(whole.shape, sub_phase.dtype)
    for tap in range(TAPS):
        matrix = jnp.where(whole == tap - 3, weights[:, tap][:, None, None], matrix)
    return matrix


def warp_batch(slab_images, row_shift, col_shift, row_phase, col_phase):
    side_len = slab_images.shape[1]
    left_matrix = lanczos_batch(row_shift, row_phase, side_len)
    middle = jnp.einsum("kia,kab->kib", left_matrix, slab_images, precision=warp_mode)
    right_matrix = lanczos_batch(col_shift, col_phase, side_len)
    return jnp.einsum("kib,kjb->kij", middle, right_matrix, precision=warp_mode)


def chebyshev_rows(first_pixel, side_len):
    pixels = (first_pixel + jnp.arange(side_len, dtype=jnp.int32)).astype(jnp.float32)
    coordinate = (2.0 * pixels + 1.0) / TILE - 1.0
    orders = jnp.arange(TERMS, dtype=jnp.int32).astype(jnp.float32)
    return jnp.cos(orders[:, None] * jnp.arccos(coordinate)[None, :])


def basis_pair(anchor_pairs, side_len):
    row_basis = jax.vmap(lambda first_pixel: chebyshev_rows(first_pixel, side_len))(
        anchor_pairs[:, 0]
    )
    col_basis = jax.vmap(lambda first_pixel: chebyshev_rows(first_pixel, side_len))(
        anchor_pairs[:, 1]
    )
    return (row_basis, col_basis)


def project_terms(differences, row_basis, col_basis):
    middle = jnp.einsum("mtp,mpq->mtq", row_basis, differences, precision=warp_mode)
    return jnp.einsum("mtq,muq->mtu", middle, col_basis, precision=exact_mode)


def ring_sum(value, axis_name):
    count = lax.axis_size(axis_name)
    me = lax.axis_index(axis_name)
    received = [value]
    for step in range(1, count):
        pairs = [(i, (i + step) % count) for i in range(count)]
        received.append(lax.ppermute(value, axis_name, pairs))
    stacked = jnp.stack(received)
    total = None
    for source in range(count):
        term = lax.dynamic_index_in_dim(stacked, (me - source) % count, 0, keepdims=False)
        total = term if total is None else total + term
    return total


def body(pieces, ref_patch, piece_patch, piece_visit, anchors, shifts, phases):
    piece_count = pieces.shape[0]
    side_len = pieces.shape[1]
    patch_count = lax.axis_size(PATCH_PARTS)
    gathered = lax.all_gather(ref_patch, PATCH_PARTS + VISIT_PARTS, axis=0, tiled=True)
    ref_block = gathered.reshape(patch_count, side_len, side_len)
    visit_slots = jnp.arange(VIS_DEV, dtype=jnp.int32)
    own_onehot = (piece_visit[:, None] == visit_slots[None, :]).astype(jnp.float32)
    warped_all = warp_batch(pieces, shifts[:, 0], shifts[:, 1], phases[:, 0], phases[:, 1])
    warped_all = lax.optimization_barrier(warped_all)
    own_diffs = warped_all - jnp.take(ref_block, piece_patch, axis=0)
    row_basis, col_basis = basis_pair(anchors, side_len)
    warp_terms = project_terms(warped_all, row_basis, col_basis)
    against_cols = jnp.einsum("qpr,kur->qpku", ref_block, col_basis, precision=warp_mode)
    picked = against_cols[piece_patch, :, jnp.arange(piece_count), :]
    ref_terms = jnp.einsum("ktp,kpu->ktu", row_basis, picked, precision=exact_mode)
    partial_value = warp_terms - ref_terms
    local_sums = jnp.einsum("kv,ktu->vtu", own_onehot, partial_value, precision=exact_mode)
    totals = ring_sum(ring_sum(local_sums, "pz"), "px")
    coefficients = totals / float(patch_count * (piece_count // VIS_DEV) * side_len * side_len)
    chosen = jnp.take(coefficients, piece_visit, axis=0)
    middle = jnp.einsum("ktp,ktu->kpu", row_basis, chosen, precision=warp_mode)
    fitted = jnp.einsum("kpu,kuq->kpq", middle, col_basis, precision=warp_mode)
    return (own_diffs - fitted, coefficients)


def solution(mesh):
    visit_size = mesh.shape["visit"]
    patch_size = mesh.shape["patch"]
    fine = Mesh(
        mesh.devices.reshape(visit_size // 2, 2, 4, patch_size // 4),
        PIECE_AXES,
    )
    return jax.shard_map(
        body,
        mesh=fine,
        in_specs=(
            P(PIECE_AXES, None, None),
            P(PATCH_PARTS, VISIT_PARTS, None),
            P(PIECE_AXES),
            P(PIECE_AXES),
            P(PIECE_AXES, None),
            P(PIECE_AXES, None),
            P(PIECE_AXES, None),
        ),
        out_specs=(P(PIECE_AXES, None, None), P(VISIT_PARTS, None, None)),
        check_vma=False,
    )
```

```python
import jax
import jax.numpy as jnp
from jax import lax
from jax.sharding import Mesh
from jax.sharding import PartitionSpec as P

VIS_DEV = 4
TERMS = 17
TILE = 4096
TAPS = 6

VISIT_PARTS = ("vy", "vc")
PATCH_PARTS = ("px", "pz")
PIECE_AXES = VISIT_PARTS + PATCH_PARTS


exact_mode = lax.Precision.HIGHEST
warp_mode = lax.Precision.HIGH


def tap_weights(sub_phase):
    distance = jnp.arange(-3, 3, dtype=jnp.int32)
    offset = distance.astype(sub_phase.dtype)[None, :] + sub_phase[:, None]
    weight = jnp.sinc(offset) * jnp.sinc(offset / 3.0)
    return jnp.where(jnp.abs(offset) < 3.0, weight, jnp.zeros_like(weight))


def lanczos_batch(band_shift, sub_phase, side_len):
    positions = jnp.arange(side_len, dtype=jnp.int32)
    whole = positions[None, :, None] + band_shift[:, None, None] - positions[None, None, :]
    weights = tap_weights(sub_phase)
    matrix = jnp.zeros(whole.shape, sub_phase.dtype)
    for tap in range(TAPS):
        matrix = jnp.where(whole == tap - 3, weights[:, tap][:, None, None], matrix)
    return matrix


def warp_batch(slab_images, row_shift, col_shift, row_phase, col_phase):
    side_len = slab_images.shape[1]
    left_matrix = lanczos_batch(row_shift, row_phase, side_len)
    middle = jnp.einsum("kia,kab->kib", left_matrix, slab_images, precision=warp_mode)
    right_matrix = lanczos_batch(col_shift, col_phase, side_len)
    return jnp.einsum("kib,kjb->kij", middle, right_matrix, precision=warp_mode)


def chebyshev_rows(first_pixel, side_len):
    pixels = (first_pixel + jnp.arange(side_len, dtype=jnp.int32)).astype(jnp.float32)
    coordinate = (2.0 * pixels + 1.0) / TILE - 1.0
    orders = jnp.arange(TERMS, dtype=jnp.int32).astype(jnp.float32)
    return jnp.cos(orders[:, None] * jnp.arccos(coordinate)[None, :])


def basis_pair(anchor_pairs, side_len):
    row_basis = jax.vmap(lambda first_pixel: chebyshev_rows(first_pixel, side_len))(
        anchor_pairs[:, 0]
    )
    col_basis = jax.vmap(lambda first_pixel: chebyshev_rows(first_pixel, side_len))(
        anchor_pairs[:, 1]
    )
    return (row_basis, col_basis)


def project_terms(differences, row_basis, col_basis):
    middle = jnp.einsum("mtp,mpq->mtq", row_basis, differences, precision=warp_mode)
    return jnp.einsum("mtq,muq->mtu", middle, col_basis, precision=exact_mode)


def ring_sum(value, axis_name):
    count = lax.axis_size(axis_name)
    me = lax.axis_index(axis_name)
    received = [value]
    for step in range(1, count):
        pairs = [(i, (i + step) % count) for i in range(count)]
        received.append(lax.ppermute(value, axis_name, pairs))
    stacked = jnp.stack(received)
    total = None
    for source in range(count):
        term = lax.dynamic_index_in_dim(stacked, (me - source) % count, 0, keepdims=False)
        total = term if total is None else total + term
    return total


def body(pieces, ref_patch, piece_patch, piece_visit, anchors, shifts, phases):
    piece_count = pieces.shape[0]
    side_len = pieces.shape[1]
    patch_count = lax.axis_size(PATCH_PARTS)
    gathered = lax.all_gather(ref_patch, PATCH_PARTS + VISIT_PARTS, axis=0, tiled=True)
    ref_block = gathered.reshape(patch_count, side_len, side_len)
    visit_slots = jnp.arange(VIS_DEV, dtype=jnp.int32)
    own_onehot = (piece_visit[:, None] == visit_slots[None, :]).astype(jnp.float32)
    warped_all = warp_batch(pieces, shifts[:, 0], shifts[:, 1], phases[:, 0], phases[:, 1])
    warped_all = lax.optimization_barrier(warped_all)
    own_diffs = warped_all - jnp.take(ref_block, piece_patch, axis=0)
    row_basis, col_basis = basis_pair(anchors, side_len)
    warp_terms = project_terms(warped_all, row_basis, col_basis)
    against_cols = jnp.einsum("qpr,kur->qpku", ref_block, col_basis, precision=lax.Precision.DEFAULT)
    picked = against_cols[piece_patch, :, jnp.arange(piece_count), :]
    ref_terms = jnp.einsum("ktp,kpu->ktu", row_basis, picked, precision=exact_mode)
    partial_value = warp_terms - ref_terms
    local_sums = jnp.einsum("kv,ktu->vtu", own_onehot, partial_value, precision=exact_mode)
    totals = ring_sum(ring_sum(local_sums, "pz"), "px")
    coefficients = totals / float(patch_count * (piece_count // VIS_DEV) * side_len * side_len)
    chosen = jnp.take(coefficients, piece_visit, axis=0)
    middle = jnp.einsum("ktp,ktu->kpu", row_basis, chosen, precision=warp_mode)
    fitted = jnp.einsum("kpu,kuq->kpq", middle, col_basis, precision=warp_mode)
    return (own_diffs - fitted, coefficients)


def solution(mesh):
    visit_size = mesh.shape["visit"]
    patch_size = mesh.shape["patch"]
    fine = Mesh(
        mesh.devices.reshape(visit_size // 2, 2, 4, patch_size // 4),
        PIECE_AXES,
    )
    return jax.shard_map(
        body,
        mesh=fine,
        in_specs=(
            P(PIECE_AXES, None, None),
            P(PATCH_PARTS, VISIT_PARTS, None),
            P(PIECE_AXES),
            P(PIECE_AXES),
            P(PIECE_AXES, None),
            P(PIECE_AXES, None),
            P(PIECE_AXES, None),
        ),
        out_specs=(P(PIECE_AXES, None, None), P(VISIT_PARTS, None, None)),
        check_vma=False,
    )
```

```python
import jax
import jax.numpy as jnp
from jax import lax
from jax.experimental import pallas as pl
from jax.experimental.pallas import tpu as pltpu
from jax.sharding import Mesh
from jax.sharding import PartitionSpec as P

VIS_DEV = 4
TERMS = 17
TILE = 4096
TAPS = 6

VISIT_PARTS = ("vy", "vc")
PATCH_PARTS = ("px", "pz")
PIECE_AXES = VISIT_PARTS + PATCH_PARTS


exact_mode = lax.Precision.HIGHEST
warp_mode = lax.Precision.HIGH


def tap_weights(sub_phase):
    distance = jnp.arange(-3, 3, dtype=jnp.int32)
    offset = distance.astype(sub_phase.dtype)[None, :] + sub_phase[:, None]
    weight = jnp.sinc(offset) * jnp.sinc(offset / 3.0)
    return jnp.where(jnp.abs(offset) < 3.0, weight, jnp.zeros_like(weight))


def lanczos_batch(band_shift, sub_phase, side_len):
    positions = jnp.arange(side_len, dtype=jnp.int32)
    whole = positions[None, :, None] + band_shift[:, None, None] - positions[None, None, :]
    weights = tap_weights(sub_phase)
    matrix = jnp.zeros(whole.shape, sub_phase.dtype)
    for tap in range(TAPS):
        matrix = jnp.where(whole == tap - 3, weights[:, tap][:, None, None], matrix)
    return matrix


def warp_batch(slab_images, row_shift, col_shift, row_phase, col_phase):
    side_len = slab_images.shape[1]
    left_matrix = lanczos_batch(row_shift, row_phase, side_len)
    middle = jnp.einsum("kia,kab->kib", left_matrix, slab_images, precision=warp_mode)
    right_matrix = lanczos_batch(col_shift, col_phase, side_len)
    return jnp.einsum("kib,kjb->kij", middle, right_matrix, precision=warp_mode)


def chebyshev_rows(first_pixel, side_len):
    pixels = (first_pixel + jnp.arange(side_len, dtype=jnp.int32)).astype(jnp.float32)
    coordinate = (2.0 * pixels + 1.0) / TILE - 1.0
    orders = jnp.arange(TERMS, dtype=jnp.int32).astype(jnp.float32)
    return jnp.cos(orders[:, None] * jnp.arccos(coordinate)[None, :])


def basis_pair(anchor_pairs, side_len):
    row_basis = jax.vmap(lambda first_pixel: chebyshev_rows(first_pixel, side_len))(
        anchor_pairs[:, 0]
    )
    col_basis = jax.vmap(lambda first_pixel: chebyshev_rows(first_pixel, side_len))(
        anchor_pairs[:, 1]
    )
    return (row_basis, col_basis)


def project_terms(differences, row_basis, col_basis):
    middle = jnp.einsum("mtp,mpq->mtq", row_basis, differences, precision=warp_mode)
    return jnp.einsum("mtq,muq->mtu", middle, col_basis, precision=exact_mode)


BASIS_ROWS = 24


def reference_terms_kernel(patch_of, ref_ref, row_ref, col_ref, out_ref):
    middle = jnp.dot(row_ref[0], ref_ref[0], preferred_element_type=jnp.float32, precision=exact_mode)
    out_ref[0] = lax.dot_general(
        middle, col_ref[0], (((1,), (1,)), ((), ())), preferred_element_type=jnp.float32, precision=exact_mode
    )


def reference_terms(ref_block, piece_patch, row_basis, col_basis):
    piece_count, terms, side_len = row_basis.shape
    pad = ((0, 0), (0, BASIS_ROWS - terms), (0, 0))
    rows = jnp.pad(row_basis, pad)
    cols = jnp.pad(col_basis, pad)
    basis_spec = pl.BlockSpec((1, BASIS_ROWS, side_len), lambda k, patch_of: (k, 0, 0))
    out = pl.pallas_call(
        reference_terms_kernel,
        out_shape=jax.ShapeDtypeStruct((piece_count, BASIS_ROWS, BASIS_ROWS), jnp.float32),
        grid_spec=pltpu.PrefetchScalarGridSpec(
            num_scalar_prefetch=1,
            grid=(piece_count,),
            in_specs=[
                pl.BlockSpec((1, side_len, side_len), lambda k, patch_of: (patch_of[k], 0, 0)),
                basis_spec,
                basis_spec,
            ],
            out_specs=pl.BlockSpec((1, BASIS_ROWS, BASIS_ROWS), lambda k, patch_of: (k, 0, 0)),
        ),
        cost_estimate=pl.CostEstimate(
            flops=2 * piece_count * BASIS_ROWS * side_len * (side_len + BASIS_ROWS),
            bytes_accessed=4 * piece_count * side_len * (side_len + 2 * BASIS_ROWS),
            transcendentals=0,
        ),
    )(piece_patch, ref_block, rows, cols)
    return out[:, :terms, :terms]


def ring_sum(value, axis_name):
    count = lax.axis_size(axis_name)
    me = lax.axis_index(axis_name)
    received = [value]
    for step in range(1, count):
        pairs = [(i, (i + step) % count) for i in range(count)]
        received.append(lax.ppermute(value, axis_name, pairs))
    stacked = jnp.stack(received)
    total = None
    for source in range(count):
        term = lax.dynamic_index_in_dim(stacked, (me - source) % count, 0, keepdims=False)
        total = term if total is None else total + term
    return total


def body(pieces, ref_patch, piece_patch, piece_visit, anchors, shifts, phases):
    piece_count = pieces.shape[0]
    side_len = pieces.shape[1]
    patch_count = lax.axis_size(PATCH_PARTS)
    gathered = lax.all_gather(ref_patch, PATCH_PARTS + VISIT_PARTS, axis=0, tiled=True)
    ref_block = gathered.reshape(patch_count, side_len, side_len)
    visit_slots = jnp.arange(VIS_DEV, dtype=jnp.int32)
    own_onehot = (piece_visit[:, None] == visit_slots[None, :]).astype(jnp.float32)
    warped_all = warp_batch(pieces, shifts[:, 0], shifts[:, 1], phases[:, 0], phases[:, 1])
    warped_all = lax.optimization_barrier(warped_all)
    own_diffs = warped_all - jnp.take(ref_block, piece_patch, axis=0)
    row_basis, col_basis = basis_pair(anchors, side_len)
    warp_terms = project_terms(warped_all, row_basis, col_basis)
    ref_terms = reference_terms(ref_block, piece_patch, row_basis, col_basis)
    partial_value = warp_terms - ref_terms
    local_sums = jnp.einsum("kv,ktu->vtu", own_onehot, partial_value, precision=exact_mode)
    totals = ring_sum(ring_sum(local_sums, "pz"), "px")
    coefficients = totals / float(patch_count * (piece_count // VIS_DEV) * side_len * side_len)
    chosen = jnp.take(coefficients, piece_visit, axis=0)
    middle = jnp.einsum("ktp,ktu->kpu", row_basis, chosen, precision=warp_mode)
    fitted = jnp.einsum("kpu,kuq->kpq", middle, col_basis, precision=warp_mode)
    return (own_diffs - fitted, coefficients)


def solution(mesh):
    visit_size = mesh.shape["visit"]
    patch_size = mesh.shape["patch"]
    fine = Mesh(
        mesh.devices.reshape(visit_size // 2, 2, 4, patch_size // 4),
        PIECE_AXES,
    )
    return jax.shard_map(
        body,
        mesh=fine,
        in_specs=(
            P(PIECE_AXES, None, None),
            P(PATCH_PARTS, VISIT_PARTS, None),
            P(PIECE_AXES),
            P(PIECE_AXES),
            P(PIECE_AXES, None),
            P(PIECE_AXES, None),
            P(PIECE_AXES, None),
        ),
        out_specs=(P(PIECE_AXES, None, None), P(VISIT_PARTS, None, None)),
        check_vma=False,
    )
```

```python
import jax
import jax.numpy as jnp
from jax import lax
from jax.experimental import pallas as pl
from jax.experimental.pallas import tpu as pltpu
from jax.sharding import Mesh
from jax.sharding import PartitionSpec as P

VIS_DEV = 4
TERMS = 17
TILE = 4096
TAPS = 6

VISIT_PARTS = ("vy", "vc")
PATCH_PARTS = ("px", "pz")
PIECE_AXES = VISIT_PARTS + PATCH_PARTS


exact_mode = lax.Precision.HIGHEST
warp_mode = lax.Precision.HIGH


def tap_weights(sub_phase):
    distance = jnp.arange(-3, 3, dtype=jnp.int32)
    offset = distance.astype(sub_phase.dtype)[None, :] + sub_phase[:, None]
    weight = jnp.sinc(offset) * jnp.sinc(offset / 3.0)
    return jnp.where(jnp.abs(offset) < 3.0, weight, jnp.zeros_like(weight))


def lanczos_batch(band_shift, sub_phase, side_len):
    positions = jnp.arange(side_len, dtype=jnp.int32)
    whole = positions[None, :, None] + band_shift[:, None, None] - positions[None, None, :]
    weights = tap_weights(sub_phase)
    matrix = jnp.zeros(whole.shape, sub_phase.dtype)
    for tap in range(TAPS):
        matrix = jnp.where(whole == tap - 3, weights[:, tap][:, None, None], matrix)
    return matrix


def warp_batch(slab_images, row_shift, col_shift, row_phase, col_phase):
    side_len = slab_images.shape[1]
    left_matrix = lanczos_batch(row_shift, row_phase, side_len)
    middle = jnp.einsum("kia,kab->kib", left_matrix, slab_images, precision=warp_mode)
    right_matrix = lanczos_batch(col_shift, col_phase, side_len)
    return jnp.einsum("kib,kjb->kij", middle, right_matrix, precision=warp_mode)


def chebyshev_rows(first_pixel, side_len):
    pixels = (first_pixel + jnp.arange(side_len, dtype=jnp.int32)).astype(jnp.float32)
    coordinate = (2.0 * pixels + 1.0) / TILE - 1.0
    orders = jnp.arange(TERMS, dtype=jnp.int32).astype(jnp.float32)
    return jnp.cos(orders[:, None] * jnp.arccos(coordinate)[None, :])


def basis_pair(anchor_pairs, side_len):
    row_basis = jax.vmap(lambda first_pixel: chebyshev_rows(first_pixel, side_len))(
        anchor_pairs[:, 0]
    )
    col_basis = jax.vmap(lambda first_pixel: chebyshev_rows(first_pixel, side_len))(
        anchor_pairs[:, 1]
    )
    return (row_basis, col_basis)


def project_terms(differences, row_basis, col_basis):
    middle = jnp.einsum("mtp,mpq->mtq", row_basis, differences, precision=warp_mode)
    return jnp.einsum("mtq,muq->mtu", middle, col_basis, precision=exact_mode)


BASIS_ROWS = 24


def reference_terms_kernel(patch_of, ref_ref, row_ref, col_ref, out_ref):
    against_cols = lax.dot_general(
        ref_ref[0], col_ref[0], (((1,), (1,)), ((), ())), preferred_element_type=jnp.float32, precision=exact_mode
    )
    out_ref[0] = jnp.dot(row_ref[0], against_cols, preferred_element_type=jnp.float32, precision=exact_mode)


def reference_terms(ref_block, piece_patch, row_basis, col_basis):
    piece_count, terms, side_len = row_basis.shape
    pad = ((0, 0), (0, BASIS_ROWS - terms), (0, 0))
    rows = jnp.pad(row_basis, pad)
    cols = jnp.pad(col_basis, pad)
    basis_spec = pl.BlockSpec((1, BASIS_ROWS, side_len), lambda k, patch_of: (k, 0, 0))
    out = pl.pallas_call(
        reference_terms_kernel,
        out_shape=jax.ShapeDtypeStruct((piece_count, BASIS_ROWS, BASIS_ROWS), jnp.float32),
        grid_spec=pltpu.PrefetchScalarGridSpec(
            num_scalar_prefetch=1,
            grid=(piece_count,),
            in_specs=[
                pl.BlockSpec((1, side_len, side_len), lambda k, patch_of: (patch_of[k], 0, 0)),
                basis_spec,
                basis_spec,
            ],
            out_specs=pl.BlockSpec((1, BASIS_ROWS, BASIS_ROWS), lambda k, patch_of: (k, 0, 0)),
        ),
        cost_estimate=pl.CostEstimate(
            flops=2 * piece_count * BASIS_ROWS * side_len * (side_len + BASIS_ROWS),
            bytes_accessed=4 * piece_count * side_len * (side_len + 2 * BASIS_ROWS),
            transcendentals=0,
        ),
    )(piece_patch, ref_block, rows, cols)
    return out[:, :terms, :terms]


def ring_sum(value, axis_name):
    count = lax.axis_size(axis_name)
    me = lax.axis_index(axis_name)
    received = [value]
    for step in range(1, count):
        pairs = [(i, (i + step) % count) for i in range(count)]
        received.append(lax.ppermute(value, axis_name, pairs))
    stacked = jnp.stack(received)
    total = None
    for source in range(count):
        term = lax.dynamic_index_in_dim(stacked, (me - source) % count, 0, keepdims=False)
        total = term if total is None else total + term
    return total


def body(pieces, ref_patch, piece_patch, piece_visit, anchors, shifts, phases):
    piece_count = pieces.shape[0]
    side_len = pieces.shape[1]
    patch_count = lax.axis_size(PATCH_PARTS)
    gathered = lax.all_gather(ref_patch, PATCH_PARTS + VISIT_PARTS, axis=0, tiled=True)
    ref_block = gathered.reshape(patch_count, side_len, side_len)
    visit_slots = jnp.arange(VIS_DEV, dtype=jnp.int32)
    own_onehot = (piece_visit[:, None] == visit_slots[None, :]).astype(jnp.float32)
    warped_all = warp_batch(pieces, shifts[:, 0], shifts[:, 1], phases[:, 0], phases[:, 1])
    warped_all = lax.optimization_barrier(warped_all)
    own_diffs = warped_all - jnp.take(ref_block, piece_patch, axis=0)
    row_basis, col_basis = basis_pair(anchors, side_len)
    warp_terms = project_terms(warped_all, row_basis, col_basis)
    ref_terms = reference_terms(ref_block, piece_patch, row_basis, col_basis)
    partial_value = warp_terms - ref_terms
    local_sums = jnp.einsum("kv,ktu->vtu", own_onehot, partial_value, precision=exact_mode)
    totals = ring_sum(ring_sum(local_sums, "pz"), "px")
    coefficients = totals / float(patch_count * (piece_count // VIS_DEV) * side_len * side_len)
    chosen = jnp.take(coefficients, piece_visit, axis=0)
    middle = jnp.einsum("ktp,ktu->kpu", row_basis, chosen, precision=warp_mode)
    fitted = jnp.einsum("kpu,kuq->kpq", middle, col_basis, precision=warp_mode)
    return (own_diffs - fitted, coefficients)


def solution(mesh):
    visit_size = mesh.shape["visit"]
    patch_size = mesh.shape["patch"]
    fine = Mesh(
        mesh.devices.reshape(visit_size // 2, 2, 4, patch_size // 4),
        PIECE_AXES,
    )
    return jax.shard_map(
        body,
        mesh=fine,
        in_specs=(
            P(PIECE_AXES, None, None),
            P(PATCH_PARTS, VISIT_PARTS, None),
            P(PIECE_AXES),
            P(PIECE_AXES),
            P(PIECE_AXES, None),
            P(PIECE_AXES, None),
            P(PIECE_AXES, None),
        ),
        out_specs=(P(PIECE_AXES, None, None), P(VISIT_PARTS, None, None)),
        check_vma=False,
    )
```

```python
import jax
import jax.numpy as jnp
from jax import lax
from jax.experimental import pallas as pl
from jax.experimental.pallas import tpu as pltpu
from jax.sharding import Mesh
from jax.sharding import PartitionSpec as P

VIS_DEV = 4
TERMS = 17
TILE = 4096
TAPS = 6

VISIT_PARTS = ("vy", "vc")
PATCH_PARTS = ("px", "pz")
PIECE_AXES = VISIT_PARTS + PATCH_PARTS


exact_mode = lax.Precision.HIGHEST
warp_mode = lax.Precision.HIGH


def tap_weights(sub_phase):
    distance = jnp.arange(-3, 3, dtype=jnp.int32)
    offset = distance.astype(sub_phase.dtype)[None, :] + sub_phase[:, None]
    weight = jnp.sinc(offset) * jnp.sinc(offset / 3.0)
    return jnp.where(jnp.abs(offset) < 3.0, weight, jnp.zeros_like(weight))


def lanczos_batch(band_shift, sub_phase, side_len):
    positions = jnp.arange(side_len, dtype=jnp.int32)
    whole = positions[None, :, None] + band_shift[:, None, None] - positions[None, None, :]
    weights = tap_weights(sub_phase)
    matrix = jnp.zeros(whole.shape, sub_phase.dtype)
    for tap in range(TAPS):
        matrix = jnp.where(whole == tap - 3, weights[:, tap][:, None, None], matrix)
    return matrix


def warp_batch(slab_images, row_shift, col_shift, row_phase, col_phase):
    side_len = slab_images.shape[1]
    left_matrix = lanczos_batch(row_shift, row_phase, side_len)
    middle = jnp.einsum("kia,kab->kib", left_matrix, slab_images, precision=warp_mode)
    right_matrix = lanczos_batch(col_shift, col_phase, side_len)
    return jnp.einsum("kib,kjb->kij", middle, right_matrix, precision=warp_mode)


def chebyshev_rows(first_pixel, side_len):
    pixels = (first_pixel + jnp.arange(side_len, dtype=jnp.int32)).astype(jnp.float32)
    coordinate = (2.0 * pixels + 1.0) / TILE - 1.0
    orders = jnp.arange(TERMS, dtype=jnp.int32).astype(jnp.float32)
    return jnp.cos(orders[:, None] * jnp.arccos(coordinate)[None, :])


def basis_pair(anchor_pairs, side_len):
    row_basis = jax.vmap(lambda first_pixel: chebyshev_rows(first_pixel, side_len))(
        anchor_pairs[:, 0]
    )
    col_basis = jax.vmap(lambda first_pixel: chebyshev_rows(first_pixel, side_len))(
        anchor_pairs[:, 1]
    )
    return (row_basis, col_basis)


def project_terms(differences, row_basis, col_basis):
    middle = jnp.einsum("mtp,mpq->mtq", row_basis, differences, precision=warp_mode)
    return jnp.einsum("mtq,muq->mtu", middle, col_basis, precision=exact_mode)


BASIS_ROWS = 24


def reference_terms_kernel(patch_of, ref_ref, row_ref, col_ref, out_ref):
    rows = row_ref[0]
    image = ref_ref[0]
    rows_high = rows.astype(jnp.bfloat16)
    rows_low = (rows - rows_high.astype(jnp.float32)).astype(jnp.bfloat16)
    image_high = image.astype(jnp.bfloat16)
    image_low = (image - image_high.astype(jnp.float32)).astype(jnp.bfloat16)
    middle = jnp.dot(rows_high, image_high, preferred_element_type=jnp.float32)
    middle = middle + jnp.dot(rows_low, image_high, preferred_element_type=jnp.float32)
    middle = middle + jnp.dot(rows_high, image_low, preferred_element_type=jnp.float32)
    out_ref[0] = lax.dot_general(
        middle, col_ref[0], (((1,), (1,)), ((), ())), preferred_element_type=jnp.float32, precision=exact_mode
    )


def reference_terms(ref_block, piece_patch, row_basis, col_basis):
    piece_count, terms, side_len = row_basis.shape
    pad = ((0, 0), (0, BASIS_ROWS - terms), (0, 0))
    rows = jnp.pad(row_basis, pad)
    cols = jnp.pad(col_basis, pad)
    basis_spec = pl.BlockSpec((1, BASIS_ROWS, side_len), lambda k, patch_of: (k, 0, 0))
    out = pl.pallas_call(
        reference_terms_kernel,
        out_shape=jax.ShapeDtypeStruct((piece_count, BASIS_ROWS, BASIS_ROWS), jnp.float32),
        grid_spec=pltpu.PrefetchScalarGridSpec(
            num_scalar_prefetch=1,
            grid=(piece_count,),
            in_specs=[
                pl.BlockSpec((1, side_len, side_len), lambda k, patch_of: (patch_of[k], 0, 0)),
                basis_spec,
                basis_spec,
            ],
            out_specs=pl.BlockSpec((1, BASIS_ROWS, BASIS_ROWS), lambda k, patch_of: (k, 0, 0)),
        ),
        cost_estimate=pl.CostEstimate(
            flops=2 * piece_count * BASIS_ROWS * side_len * (side_len + BASIS_ROWS),
            bytes_accessed=4 * piece_count * side_len * (side_len + 2 * BASIS_ROWS),
            transcendentals=0,
        ),
    )(piece_patch, ref_block, rows, cols)
    return out[:, :terms, :terms]


def ring_sum(value, axis_name):
    count = lax.axis_size(axis_name)
    me = lax.axis_index(axis_name)
    received = [value]
    for step in range(1, count):
        pairs = [(i, (i + step) % count) for i in range(count)]
        received.append(lax.ppermute(value, axis_name, pairs))
    stacked = jnp.stack(received)
    total = None
    for source in range(count):
        term = lax.dynamic_index_in_dim(stacked, (me - source) % count, 0, keepdims=False)
        total = term if total is None else total + term
    return total


def body(pieces, ref_patch, piece_patch, piece_visit, anchors, shifts, phases):
    piece_count = pieces.shape[0]
    side_len = pieces.shape[1]
    patch_count = lax.axis_size(PATCH_PARTS)
    gathered = lax.all_gather(ref_patch, PATCH_PARTS + VISIT_PARTS, axis=0, tiled=True)
    ref_block = gathered.reshape(patch_count, side_len, side_len)
    visit_slots = jnp.arange(VIS_DEV, dtype=jnp.int32)
    own_onehot = (piece_visit[:, None] == visit_slots[None, :]).astype(jnp.float32)
    warped_all = warp_batch(pieces, shifts[:, 0], shifts[:, 1], phases[:, 0], phases[:, 1])
    warped_all = lax.optimization_barrier(warped_all)
    own_diffs = warped_all - jnp.take(ref_block, piece_patch, axis=0)
    row_basis, col_basis = basis_pair(anchors, side_len)
    warp_terms = project_terms(warped_all, row_basis, col_basis)
    ref_terms = reference_terms(ref_block, piece_patch, row_basis, col_basis)
    partial_value = warp_terms - ref_terms
    local_sums = jnp.einsum("kv,ktu->vtu", own_onehot, partial_value, precision=exact_mode)
    totals = ring_sum(ring_sum(local_sums, "pz"), "px")
    coefficients = totals / float(patch_count * (piece_count // VIS_DEV) * side_len * side_len)
    chosen = jnp.take(coefficients, piece_visit, axis=0)
    middle = jnp.einsum("ktp,ktu->kpu", row_basis, chosen, precision=warp_mode)
    fitted = jnp.einsum("kpu,kuq->kpq", middle, col_basis, precision=warp_mode)
    return (own_diffs - fitted, coefficients)


def solution(mesh):
    visit_size = mesh.shape["visit"]
    patch_size = mesh.shape["patch"]
    fine = Mesh(
        mesh.devices.reshape(visit_size // 2, 2, 4, patch_size // 4),
        PIECE_AXES,
    )
    return jax.shard_map(
        body,
        mesh=fine,
        in_specs=(
            P(PIECE_AXES, None, None),
            P(PATCH_PARTS, VISIT_PARTS, None),
            P(PIECE_AXES),
            P(PIECE_AXES),
            P(PIECE_AXES, None),
            P(PIECE_AXES, None),
            P(PIECE_AXES, None),
        ),
        out_specs=(P(PIECE_AXES, None, None), P(VISIT_PARTS, None, None)),
        check_vma=False,
    )
```

```python
import jax
import jax.numpy as jnp
from jax import lax
from jax.experimental import pallas as pl
from jax.experimental.pallas import tpu as pltpu
from jax.sharding import Mesh
from jax.sharding import PartitionSpec as P

VIS_DEV = 4
TERMS = 17
TILE = 4096
TAPS = 6

VISIT_PARTS = ("vy", "vc")
PATCH_PARTS = ("px", "pz")
PIECE_AXES = VISIT_PARTS + PATCH_PARTS


exact_mode = lax.Precision.HIGHEST
warp_mode = lax.Precision.HIGH


def tap_weights(sub_phase):
    distance = jnp.arange(-3, 3, dtype=jnp.int32)
    offset = distance.astype(sub_phase.dtype)[None, :] + sub_phase[:, None]
    weight = jnp.sinc(offset) * jnp.sinc(offset / 3.0)
    return jnp.where(jnp.abs(offset) < 3.0, weight, jnp.zeros_like(weight))


def lanczos_batch(band_shift, sub_phase, side_len):
    positions = jnp.arange(side_len, dtype=jnp.int32)
    whole = positions[None, :, None] + band_shift[:, None, None] - positions[None, None, :]
    weights = tap_weights(sub_phase)
    matrix = jnp.zeros(whole.shape, sub_phase.dtype)
    for tap in range(TAPS):
        matrix = jnp.where(whole == tap - 3, weights[:, tap][:, None, None], matrix)
    return matrix


def warp_batch(slab_images, row_shift, col_shift, row_phase, col_phase):
    side_len = slab_images.shape[1]
    left_matrix = lanczos_batch(row_shift, row_phase, side_len)
    middle = jnp.einsum("kia,kab->kib", left_matrix, slab_images, precision=warp_mode)
    right_matrix = lanczos_batch(col_shift, col_phase, side_len)
    return jnp.einsum("kib,kjb->kij", middle, right_matrix, precision=warp_mode)


def chebyshev_rows(first_pixel, side_len):
    pixels = (first_pixel + jnp.arange(side_len, dtype=jnp.int32)).astype(jnp.float32)
    coordinate = (2.0 * pixels + 1.0) / TILE - 1.0
    orders = jnp.arange(TERMS, dtype=jnp.int32).astype(jnp.float32)
    return jnp.cos(orders[:, None] * jnp.arccos(coordinate)[None, :])


def basis_pair(anchor_pairs, side_len):
    row_basis = jax.vmap(lambda first_pixel: chebyshev_rows(first_pixel, side_len))(
        anchor_pairs[:, 0]
    )
    col_basis = jax.vmap(lambda first_pixel: chebyshev_rows(first_pixel, side_len))(
        anchor_pairs[:, 1]
    )
    return (row_basis, col_basis)


def project_terms(differences, row_basis, col_basis):
    middle = jnp.einsum("mtp,mpq->mtq", row_basis, differences, precision=warp_mode)
    return jnp.einsum("mtq,muq->mtu", middle, col_basis, precision=exact_mode)


BASIS_ROWS = 24


def reference_terms_kernel(patch_of, ref_ref, row_ref, col_ref, out_ref):
    rows = row_ref[0]
    image = ref_ref[0]
    rows_high = rows.astype(jnp.bfloat16)
    rows_low = (rows - rows_high.astype(jnp.float32)).astype(jnp.bfloat16)
    image_high = image.astype(jnp.bfloat16)
    image_low = (image - image_high.astype(jnp.float32)).astype(jnp.bfloat16)
    middle = jnp.dot(rows_high, image_high, preferred_element_type=jnp.float32)
    middle = middle + jnp.dot(rows_low, image_high, preferred_element_type=jnp.float32)
    middle = middle + jnp.dot(rows_high, image_low, preferred_element_type=jnp.float32)
    out_ref[0] = lax.dot_general(
        middle, col_ref[0], (((1,), (1,)), ((), ())), preferred_element_type=jnp.float32, precision=exact_mode
    )


def reference_terms(ref_block, piece_patch, row_basis, col_basis):
    piece_count, terms, side_len = row_basis.shape
    pad = ((0, 0), (0, BASIS_ROWS - terms), (0, 0))
    rows = jnp.pad(row_basis, pad)
    cols = jnp.pad(col_basis, pad)
    basis_spec = pl.BlockSpec((1, BASIS_ROWS, side_len), lambda k, patch_of: (k, 0, 0))
    out = pl.pallas_call(
        reference_terms_kernel,
        out_shape=jax.ShapeDtypeStruct((piece_count, BASIS_ROWS, BASIS_ROWS), jnp.float32),
        grid_spec=pltpu.PrefetchScalarGridSpec(
            num_scalar_prefetch=1,
            grid=(piece_count,),
            in_specs=[
                pl.BlockSpec((1, side_len, side_len), lambda k, patch_of: (patch_of[k], 0, 0)),
                basis_spec,
                basis_spec,
            ],
            out_specs=pl.BlockSpec((1, BASIS_ROWS, BASIS_ROWS), lambda k, patch_of: (k, 0, 0)),
        ),
        cost_estimate=pl.CostEstimate(
            flops=2 * piece_count * BASIS_ROWS * side_len * (side_len + BASIS_ROWS),
            bytes_accessed=4 * piece_count * side_len * (side_len + 2 * BASIS_ROWS),
            transcendentals=0,
        ),
    )(piece_patch, ref_block, rows, cols)
    return out[:, :terms, :terms]


def matched_kernel(patch_of, warped_ref, ref_ref, rows_ref, coef_ref, col_ref, out_ref):
    middle = jnp.dot(rows_ref[0], coef_ref[0], preferred_element_type=jnp.float32, precision=exact_mode)
    fitted = jnp.dot(middle, col_ref[0], preferred_element_type=jnp.float32, precision=exact_mode)
    out_ref[0] = (warped_ref[0] - ref_ref[0]) - fitted


def matched_pieces(warped_all, ref_block, piece_patch, row_basis, chosen, col_basis):
    piece_count, terms, side_len = row_basis.shape
    extra = BASIS_ROWS - terms
    rows = jnp.pad(jnp.transpose(row_basis, (0, 2, 1)), ((0, 0), (0, 0), (0, extra)))
    coefs = jnp.pad(chosen, ((0, 0), (0, extra), (0, extra)))
    cols = jnp.pad(col_basis, ((0, 0), (0, extra), (0, 0)))
    image_spec = pl.BlockSpec((1, side_len, side_len), lambda k, patch_of: (k, 0, 0))
    return pl.pallas_call(
        matched_kernel,
        out_shape=jax.ShapeDtypeStruct(warped_all.shape, jnp.float32),
        grid_spec=pltpu.PrefetchScalarGridSpec(
            num_scalar_prefetch=1,
            grid=(piece_count,),
            in_specs=[
                image_spec,
                pl.BlockSpec((1, side_len, side_len), lambda k, patch_of: (patch_of[k], 0, 0)),
                pl.BlockSpec((1, side_len, BASIS_ROWS), lambda k, patch_of: (k, 0, 0)),
                pl.BlockSpec((1, BASIS_ROWS, BASIS_ROWS), lambda k, patch_of: (k, 0, 0)),
                pl.BlockSpec((1, BASIS_ROWS, side_len), lambda k, patch_of: (k, 0, 0)),
            ],
            out_specs=image_spec,
        ),
        cost_estimate=pl.CostEstimate(
            flops=2 * piece_count * side_len * BASIS_ROWS * (side_len + BASIS_ROWS),
            bytes_accessed=12 * piece_count * side_len * side_len,
            transcendentals=0,
        ),
    )(piece_patch, warped_all, ref_block, rows, coefs, cols)


def ring_sum(value, axis_name):
    count = lax.axis_size(axis_name)
    me = lax.axis_index(axis_name)
    received = [value]
    for step in range(1, count):
        pairs = [(i, (i + step) % count) for i in range(count)]
        received.append(lax.ppermute(value, axis_name, pairs))
    stacked = jnp.stack(received)
    total = None
    for source in range(count):
        term = lax.dynamic_index_in_dim(stacked, (me - source) % count, 0, keepdims=False)
        total = term if total is None else total + term
    return total


def body(pieces, ref_patch, piece_patch, piece_visit, anchors, shifts, phases):
    piece_count = pieces.shape[0]
    side_len = pieces.shape[1]
    patch_count = lax.axis_size(PATCH_PARTS)
    gathered = lax.all_gather(ref_patch, PATCH_PARTS + VISIT_PARTS, axis=0, tiled=True)
    ref_block = gathered.reshape(patch_count, side_len, side_len)
    visit_slots = jnp.arange(VIS_DEV, dtype=jnp.int32)
    own_onehot = (piece_visit[:, None] == visit_slots[None, :]).astype(jnp.float32)
    warped_all = warp_batch(pieces, shifts[:, 0], shifts[:, 1], phases[:, 0], phases[:, 1])
    warped_all = lax.optimization_barrier(warped_all)
    row_basis, col_basis = basis_pair(anchors, side_len)
    warp_terms = project_terms(warped_all, row_basis, col_basis)
    ref_terms = reference_terms(ref_block, piece_patch, row_basis, col_basis)
    partial_value = warp_terms - ref_terms
    local_sums = jnp.einsum("kv,ktu->vtu", own_onehot, partial_value, precision=exact_mode)
    totals = ring_sum(ring_sum(local_sums, "pz"), "px")
    coefficients = totals / float(patch_count * (piece_count // VIS_DEV) * side_len * side_len)
    chosen = jnp.take(coefficients, piece_visit, axis=0)
    matched = matched_pieces(warped_all, ref_block, piece_patch, row_basis, chosen, col_basis)
    return (matched, coefficients)


def solution(mesh):
    visit_size = mesh.shape["visit"]
    patch_size = mesh.shape["patch"]
    fine = Mesh(
        mesh.devices.reshape(visit_size // 2, 2, 4, patch_size // 4),
        PIECE_AXES,
    )
    return jax.shard_map(
        body,
        mesh=fine,
        in_specs=(
            P(PIECE_AXES, None, None),
            P(PATCH_PARTS, VISIT_PARTS, None),
            P(PIECE_AXES),
            P(PIECE_AXES),
            P(PIECE_AXES, None),
            P(PIECE_AXES, None),
            P(PIECE_AXES, None),
        ),
        out_specs=(P(PIECE_AXES, None, None), P(VISIT_PARTS, None, None)),
        check_vma=False,
    )
```

```python
import jax
import jax.numpy as jnp
from jax import lax
from jax.experimental import pallas as pl
from jax.experimental.pallas import tpu as pltpu
from jax.sharding import Mesh
from jax.sharding import PartitionSpec as P

VIS_DEV = 4
TERMS = 17
TILE = 4096
TAPS = 6

VISIT_PARTS = ("vy", "vc")
PATCH_PARTS = ("px", "pz")
PIECE_AXES = VISIT_PARTS + PATCH_PARTS


exact_mode = lax.Precision.HIGHEST
warp_mode = lax.Precision.HIGH


def tap_weights(sub_phase):
    distance = jnp.arange(-3, 3, dtype=jnp.int32)
    offset = distance.astype(sub_phase.dtype)[None, :] + sub_phase[:, None]
    weight = jnp.sinc(offset) * jnp.sinc(offset / 3.0)
    return jnp.where(jnp.abs(offset) < 3.0, weight, jnp.zeros_like(weight))


def lanczos_batch(band_shift, sub_phase, side_len):
    positions = jnp.arange(side_len, dtype=jnp.int32)
    whole = positions[None, :, None] + band_shift[:, None, None] - positions[None, None, :]
    weights = tap_weights(sub_phase)
    matrix = jnp.zeros(whole.shape, sub_phase.dtype)
    for tap in range(TAPS):
        matrix = jnp.where(whole == tap - 3, weights[:, tap][:, None, None], matrix)
    return matrix


def warp_batch(slab_images, row_shift, col_shift, row_phase, col_phase):
    side_len = slab_images.shape[1]
    left_matrix = lanczos_batch(row_shift, row_phase, side_len)
    middle = jnp.einsum("kia,kab->kib", left_matrix, slab_images, precision=warp_mode)
    right_matrix = lanczos_batch(col_shift, col_phase, side_len)
    return jnp.einsum("kib,kjb->kij", middle, right_matrix, precision=warp_mode)


def chebyshev_rows(first_pixel, side_len):
    pixels = (first_pixel + jnp.arange(side_len, dtype=jnp.int32)).astype(jnp.float32)
    coordinate = (2.0 * pixels + 1.0) / TILE - 1.0
    orders = jnp.arange(TERMS, dtype=jnp.int32).astype(jnp.float32)
    return jnp.cos(orders[:, None] * jnp.arccos(coordinate)[None, :])


def basis_pair(anchor_pairs, side_len):
    row_basis = jax.vmap(lambda first_pixel: chebyshev_rows(first_pixel, side_len))(
        anchor_pairs[:, 0]
    )
    col_basis = jax.vmap(lambda first_pixel: chebyshev_rows(first_pixel, side_len))(
        anchor_pairs[:, 1]
    )
    return (row_basis, col_basis)


def project_terms(differences, row_basis, col_basis):
    middle = jnp.einsum("mtp,mpq->mtq", row_basis, differences, precision=warp_mode)
    return jnp.einsum("mtq,muq->mtu", middle, col_basis, precision=exact_mode)


BASIS_ROWS = 24


def reference_terms_kernel(patch_of, ref_ref, row_ref, col_ref, out_ref):
    rows = row_ref[0]
    image = ref_ref[0]
    rows_high = rows.astype(jnp.bfloat16)
    rows_low = (rows - rows_high.astype(jnp.float32)).astype(jnp.bfloat16)
    image_high = image.astype(jnp.bfloat16)
    image_low = (image - image_high.astype(jnp.float32)).astype(jnp.bfloat16)
    middle = jnp.dot(rows_high, image_high, preferred_element_type=jnp.float32)
    middle = middle + jnp.dot(rows_low, image_high, preferred_element_type=jnp.float32)
    middle = middle + jnp.dot(rows_high, image_low, preferred_element_type=jnp.float32)
    out_ref[0] = lax.dot_general(
        middle, col_ref[0], (((1,), (1,)), ((), ())), preferred_element_type=jnp.float32, precision=exact_mode
    )


def reference_terms(ref_block, piece_patch, row_basis, col_basis):
    piece_count, terms, side_len = row_basis.shape
    pad = ((0, 0), (0, BASIS_ROWS - terms), (0, 0))
    rows = jnp.pad(row_basis, pad)
    cols = jnp.pad(col_basis, pad)
    basis_spec = pl.BlockSpec((1, BASIS_ROWS, side_len), lambda k, patch_of: (k, 0, 0))
    out = pl.pallas_call(
        reference_terms_kernel,
        out_shape=jax.ShapeDtypeStruct((piece_count, BASIS_ROWS, BASIS_ROWS), jnp.float32),
        grid_spec=pltpu.PrefetchScalarGridSpec(
            num_scalar_prefetch=1,
            grid=(piece_count,),
            in_specs=[
                pl.BlockSpec((1, side_len, side_len), lambda k, patch_of: (patch_of[k], 0, 0)),
                basis_spec,
                basis_spec,
            ],
            out_specs=pl.BlockSpec((1, BASIS_ROWS, BASIS_ROWS), lambda k, patch_of: (k, 0, 0)),
        ),
        cost_estimate=pl.CostEstimate(
            flops=2 * piece_count * BASIS_ROWS * side_len * (side_len + BASIS_ROWS),
            bytes_accessed=4 * piece_count * side_len * (side_len + 2 * BASIS_ROWS),
            transcendentals=0,
        ),
    )(piece_patch, ref_block, rows, cols)
    return out[:, :terms, :terms]


def matched_kernel(patch_of, warped_ref, ref_ref, rows_ref, coef_ref, col_ref, out_ref):
    middle = jnp.dot(rows_ref[0], coef_ref[0], preferred_element_type=jnp.float32, precision=exact_mode)
    cols = col_ref[0]
    middle_high = middle.astype(jnp.bfloat16)
    middle_low = (middle - middle_high.astype(jnp.float32)).astype(jnp.bfloat16)
    cols_high = cols.astype(jnp.bfloat16)
    cols_low = (cols - cols_high.astype(jnp.float32)).astype(jnp.bfloat16)
    fitted = jnp.dot(middle_high, cols_high, preferred_element_type=jnp.float32)
    fitted = fitted + jnp.dot(middle_low, cols_high, preferred_element_type=jnp.float32)
    fitted = fitted + jnp.dot(middle_high, cols_low, preferred_element_type=jnp.float32)
    out_ref[0] = (warped_ref[0] - ref_ref[0]) - fitted


def matched_pieces(warped_all, ref_block, piece_patch, row_basis, chosen, col_basis):
    piece_count, terms, side_len = row_basis.shape
    extra = BASIS_ROWS - terms
    rows = jnp.pad(jnp.transpose(row_basis, (0, 2, 1)), ((0, 0), (0, 0), (0, extra)))
    coefs = jnp.pad(chosen, ((0, 0), (0, extra), (0, extra)))
    cols = jnp.pad(col_basis, ((0, 0), (0, extra), (0, 0)))
    image_spec = pl.BlockSpec((1, side_len, side_len), lambda k, patch_of: (k, 0, 0))
    return pl.pallas_call(
        matched_kernel,
        out_shape=jax.ShapeDtypeStruct(warped_all.shape, jnp.float32),
        grid_spec=pltpu.PrefetchScalarGridSpec(
            num_scalar_prefetch=1,
            grid=(piece_count,),
            in_specs=[
                image_spec,
                pl.BlockSpec((1, side_len, side_len), lambda k, patch_of: (patch_of[k], 0, 0)),
                pl.BlockSpec((1, side_len, BASIS_ROWS), lambda k, patch_of: (k, 0, 0)),
                pl.BlockSpec((1, BASIS_ROWS, BASIS_ROWS), lambda k, patch_of: (k, 0, 0)),
                pl.BlockSpec((1, BASIS_ROWS, side_len), lambda k, patch_of: (k, 0, 0)),
            ],
            out_specs=image_spec,
        ),
        cost_estimate=pl.CostEstimate(
            flops=2 * piece_count * side_len * BASIS_ROWS * (side_len + BASIS_ROWS),
            bytes_accessed=12 * piece_count * side_len * side_len,
            transcendentals=0,
        ),
    )(piece_patch, warped_all, ref_block, rows, coefs, cols)


def ring_sum(value, axis_name):
    count = lax.axis_size(axis_name)
    me = lax.axis_index(axis_name)
    received = [value]
    for step in range(1, count):
        pairs = [(i, (i + step) % count) for i in range(count)]
        received.append(lax.ppermute(value, axis_name, pairs))
    stacked = jnp.stack(received)
    total = None
    for source in range(count):
        term = lax.dynamic_index_in_dim(stacked, (me - source) % count, 0, keepdims=False)
        total = term if total is None else total + term
    return total


def body(pieces, ref_patch, piece_patch, piece_visit, anchors, shifts, phases):
    piece_count = pieces.shape[0]
    side_len = pieces.shape[1]
    patch_count = lax.axis_size(PATCH_PARTS)
    gathered = lax.all_gather(ref_patch, PATCH_PARTS + VISIT_PARTS, axis=0, tiled=True)
    ref_block = gathered.reshape(patch_count, side_len, side_len)
    visit_slots = jnp.arange(VIS_DEV, dtype=jnp.int32)
    own_onehot = (piece_visit[:, None] == visit_slots[None, :]).astype(jnp.float32)
    warped_all = warp_batch(pieces, shifts[:, 0], shifts[:, 1], phases[:, 0], phases[:, 1])
    warped_all = lax.optimization_barrier(warped_all)
    row_basis, col_basis = basis_pair(anchors, side_len)
    warp_terms = project_terms(warped_all, row_basis, col_basis)
    ref_terms = reference_terms(ref_block, piece_patch, row_basis, col_basis)
    partial_value = warp_terms - ref_terms
    local_sums = jnp.einsum("kv,ktu->vtu", own_onehot, partial_value, precision=exact_mode)
    totals = ring_sum(ring_sum(local_sums, "pz"), "px")
    coefficients = totals / float(patch_count * (piece_count // VIS_DEV) * side_len * side_len)
    chosen = jnp.take(coefficients, piece_visit, axis=0)
    matched = matched_pieces(warped_all, ref_block, piece_patch, row_basis, chosen, col_basis)
    return (matched, coefficients)


def solution(mesh):
    visit_size = mesh.shape["visit"]
    patch_size = mesh.shape["patch"]
    fine = Mesh(
        mesh.devices.reshape(visit_size // 2, 2, 4, patch_size // 4),
        PIECE_AXES,
    )
    return jax.shard_map(
        body,
        mesh=fine,
        in_specs=(
            P(PIECE_AXES, None, None),
            P(PATCH_PARTS, VISIT_PARTS, None),
            P(PIECE_AXES),
            P(PIECE_AXES),
            P(PIECE_AXES, None),
            P(PIECE_AXES, None),
            P(PIECE_AXES, None),
        ),
        out_specs=(P(PIECE_AXES, None, None), P(VISIT_PARTS, None, None)),
        check_vma=False,
    )
```

```python
import jax
import jax.numpy as jnp
from jax import lax
from jax.experimental import pallas as pl
from jax.experimental.pallas import tpu as pltpu
from jax.sharding import Mesh
from jax.sharding import PartitionSpec as P

VIS_DEV = 4
TERMS = 17
TILE = 4096
TAPS = 6

VISIT_PARTS = ("vy", "vc")
PATCH_PARTS = ("px", "pz")
PIECE_AXES = VISIT_PARTS + PATCH_PARTS


exact_mode = lax.Precision.HIGHEST
warp_mode = lax.Precision.HIGH


def tap_weights(sub_phase):
    distance = jnp.arange(-3, 3, dtype=jnp.int32)
    offset = distance.astype(sub_phase.dtype)[None, :] + sub_phase[:, None]
    weight = jnp.sinc(offset) * jnp.sinc(offset / 3.0)
    return jnp.where(jnp.abs(offset) < 3.0, weight, jnp.zeros_like(weight))


def lanczos_batch(band_shift, sub_phase, side_len):
    positions = jnp.arange(side_len, dtype=jnp.int32)
    whole = positions[None, :, None] + band_shift[:, None, None] - positions[None, None, :]
    weights = tap_weights(sub_phase)
    matrix = jnp.zeros(whole.shape, sub_phase.dtype)
    for tap in range(TAPS):
        matrix = jnp.where(whole == tap - 3, weights[:, tap][:, None, None], matrix)
    return matrix


def warp_batch(slab_images, row_shift, col_shift, row_phase, col_phase):
    side_len = slab_images.shape[1]
    left_matrix = lanczos_batch(row_shift, row_phase, side_len)
    middle = jnp.einsum("kia,kab->kib", left_matrix, slab_images, precision=warp_mode)
    right_matrix = lanczos_batch(col_shift, col_phase, side_len)
    return jnp.einsum("kib,kjb->kij", middle, right_matrix, precision=warp_mode)


def chebyshev_rows(first_pixel, side_len):
    pixels = (first_pixel + jnp.arange(side_len, dtype=jnp.int32)).astype(jnp.float32)
    coordinate = (2.0 * pixels + 1.0) / TILE - 1.0
    orders = jnp.arange(TERMS, dtype=jnp.int32).astype(jnp.float32)
    return jnp.cos(orders[:, None] * jnp.arccos(coordinate)[None, :])


def basis_pair(anchor_pairs, side_len):
    row_basis = jax.vmap(lambda first_pixel: chebyshev_rows(first_pixel, side_len))(
        anchor_pairs[:, 0]
    )
    col_basis = jax.vmap(lambda first_pixel: chebyshev_rows(first_pixel, side_len))(
        anchor_pairs[:, 1]
    )
    return (row_basis, col_basis)


def project_terms(differences, row_basis, col_basis):
    middle = jnp.einsum("mtp,mpq->mtq", row_basis, differences, precision=warp_mode)
    return jnp.einsum("mtq,muq->mtu", middle, col_basis, precision=exact_mode)


BASIS_ROWS = 24


def reference_terms_kernel(patch_of, ref_ref, row_ref, col_ref, out_ref):
    rows = row_ref[0]
    image = ref_ref[0]
    rows_high = rows.astype(jnp.bfloat16)
    rows_low = (rows - rows_high.astype(jnp.float32)).astype(jnp.bfloat16)
    image_high = image.astype(jnp.bfloat16)
    image_low = (image - image_high.astype(jnp.float32)).astype(jnp.bfloat16)
    middle = jnp.dot(rows_high, image_high, preferred_element_type=jnp.float32)
    middle = middle + jnp.dot(rows_low, image_high, preferred_element_type=jnp.float32)
    middle = middle + jnp.dot(rows_high, image_low, preferred_element_type=jnp.float32)
    out_ref[0] = lax.dot_general(
        middle, col_ref[0], (((1,), (1,)), ((), ())), preferred_element_type=jnp.float32, precision=exact_mode
    )


def reference_terms(ref_block, piece_patch, row_basis, col_basis):
    piece_count, terms, side_len = row_basis.shape
    pad = ((0, 0), (0, BASIS_ROWS - terms), (0, 0))
    rows = jnp.pad(row_basis, pad)
    cols = jnp.pad(col_basis, pad)
    basis_spec = pl.BlockSpec((1, BASIS_ROWS, side_len), lambda k, patch_of: (k, 0, 0))
    out = pl.pallas_call(
        reference_terms_kernel,
        out_shape=jax.ShapeDtypeStruct((piece_count, BASIS_ROWS, BASIS_ROWS), jnp.float32),
        grid_spec=pltpu.PrefetchScalarGridSpec(
            num_scalar_prefetch=1,
            grid=(piece_count,),
            in_specs=[
                pl.BlockSpec((1, side_len, side_len), lambda k, patch_of: (patch_of[k], 0, 0)),
                basis_spec,
                basis_spec,
            ],
            out_specs=pl.BlockSpec((1, BASIS_ROWS, BASIS_ROWS), lambda k, patch_of: (k, 0, 0)),
        ),
        cost_estimate=pl.CostEstimate(
            flops=2 * piece_count * BASIS_ROWS * side_len * (side_len + BASIS_ROWS),
            bytes_accessed=4 * piece_count * side_len * (side_len + 2 * BASIS_ROWS),
            transcendentals=0,
        ),
    )(piece_patch, ref_block, rows, cols)
    return out[:, :terms, :terms]


def matched_kernel(patch_of, warped_ref, ref_ref, rows_ref, coef_ref, col_ref, out_ref):
    middle = jnp.dot(rows_ref[0], coef_ref[0], preferred_element_type=jnp.float32, precision=exact_mode)
    cols = col_ref[0]
    middle_high = middle.astype(jnp.bfloat16)
    middle_low = (middle - middle_high.astype(jnp.float32)).astype(jnp.bfloat16)
    cols_high = cols.astype(jnp.bfloat16)
    cols_low = (cols - cols_high.astype(jnp.float32)).astype(jnp.bfloat16)
    fitted = jnp.dot(middle_high, cols_high, preferred_element_type=jnp.float32)
    fitted = fitted + jnp.dot(middle_low, cols_high, preferred_element_type=jnp.float32)
    fitted = fitted + jnp.dot(middle_high, cols_low, preferred_element_type=jnp.float32)
    out_ref[0] = (warped_ref[0] - ref_ref[0]) - fitted


def matched_pieces(warped_all, ref_block, piece_patch, row_basis, chosen, col_basis):
    piece_count, terms, side_len = row_basis.shape
    rows = jnp.transpose(row_basis, (0, 2, 1))
    coefs = chosen
    cols = col_basis
    image_spec = pl.BlockSpec((1, side_len, side_len), lambda k, patch_of: (k, 0, 0))
    return pl.pallas_call(
        matched_kernel,
        out_shape=jax.ShapeDtypeStruct(warped_all.shape, jnp.float32),
        grid_spec=pltpu.PrefetchScalarGridSpec(
            num_scalar_prefetch=1,
            grid=(piece_count,),
            in_specs=[
                image_spec,
                pl.BlockSpec((1, side_len, side_len), lambda k, patch_of: (patch_of[k], 0, 0)),
                pl.BlockSpec((1, side_len, terms), lambda k, patch_of: (k, 0, 0)),
                pl.BlockSpec((1, terms, terms), lambda k, patch_of: (k, 0, 0)),
                pl.BlockSpec((1, terms, side_len), lambda k, patch_of: (k, 0, 0)),
            ],
            out_specs=image_spec,
        ),
        cost_estimate=pl.CostEstimate(
            flops=2 * piece_count * side_len * BASIS_ROWS * (side_len + BASIS_ROWS),
            bytes_accessed=12 * piece_count * side_len * side_len,
            transcendentals=0,
        ),
    )(piece_patch, warped_all, ref_block, rows, coefs, cols)


def ring_sum(value, axis_name):
    count = lax.axis_size(axis_name)
    me = lax.axis_index(axis_name)
    received = [value]
    for step in range(1, count):
        pairs = [(i, (i + step) % count) for i in range(count)]
        received.append(lax.ppermute(value, axis_name, pairs))
    stacked = jnp.stack(received)
    total = None
    for source in range(count):
        term = lax.dynamic_index_in_dim(stacked, (me - source) % count, 0, keepdims=False)
        total = term if total is None else total + term
    return total


def body(pieces, ref_patch, piece_patch, piece_visit, anchors, shifts, phases):
    piece_count = pieces.shape[0]
    side_len = pieces.shape[1]
    patch_count = lax.axis_size(PATCH_PARTS)
    gathered = lax.all_gather(ref_patch, PATCH_PARTS + VISIT_PARTS, axis=0, tiled=True)
    ref_block = gathered.reshape(patch_count, side_len, side_len)
    visit_slots = jnp.arange(VIS_DEV, dtype=jnp.int32)
    own_onehot = (piece_visit[:, None] == visit_slots[None, :]).astype(jnp.float32)
    warped_all = warp_batch(pieces, shifts[:, 0], shifts[:, 1], phases[:, 0], phases[:, 1])
    warped_all = lax.optimization_barrier(warped_all)
    row_basis, col_basis = basis_pair(anchors, side_len)
    warp_terms = project_terms(warped_all, row_basis, col_basis)
    ref_terms = reference_terms(ref_block, piece_patch, row_basis, col_basis)
    partial_value = warp_terms - ref_terms
    local_sums = jnp.einsum("kv,ktu->vtu", own_onehot, partial_value, precision=exact_mode)
    totals = ring_sum(ring_sum(local_sums, "pz"), "px")
    coefficients = totals / float(patch_count * (piece_count // VIS_DEV) * side_len * side_len)
    chosen = jnp.take(coefficients, piece_visit, axis=0)
    matched = matched_pieces(warped_all, ref_block, piece_patch, row_basis, chosen, col_basis)
    return (matched, coefficients)


def solution(mesh):
    visit_size = mesh.shape["visit"]
    patch_size = mesh.shape["patch"]
    fine = Mesh(
        mesh.devices.reshape(visit_size // 2, 2, 4, patch_size // 4),
        PIECE_AXES,
    )
    return jax.shard_map(
        body,
        mesh=fine,
        in_specs=(
            P(PIECE_AXES, None, None),
            P(PATCH_PARTS, VISIT_PARTS, None),
            P(PIECE_AXES),
            P(PIECE_AXES),
            P(PIECE_AXES, None),
            P(PIECE_AXES, None),
            P(PIECE_AXES, None),
        ),
        out_specs=(P(PIECE_AXES, None, None), P(VISIT_PARTS, None, None)),
        check_vma=False,
    )
```

```python
import jax
import jax.numpy as jnp
from jax import lax
from jax.experimental import pallas as pl
from jax.experimental.pallas import tpu as pltpu
from jax.sharding import Mesh
from jax.sharding import PartitionSpec as P

VIS_DEV = 4
TERMS = 17
TILE = 4096
TAPS = 6

VISIT_PARTS = ("vy", "vc")
PATCH_PARTS = ("px", "pz")
PIECE_AXES = VISIT_PARTS + PATCH_PARTS


exact_mode = lax.Precision.HIGHEST
warp_mode = lax.Precision.HIGH


def tap_weights(sub_phase):
    distance = jnp.arange(-3, 3, dtype=jnp.int32)
    offset = distance.astype(sub_phase.dtype)[None, :] + sub_phase[:, None]
    weight = jnp.sinc(offset) * jnp.sinc(offset / 3.0)
    return jnp.where(jnp.abs(offset) < 3.0, weight, jnp.zeros_like(weight))


def lanczos_batch(band_shift, sub_phase, side_len):
    positions = jnp.arange(side_len, dtype=jnp.int32)
    whole = positions[None, :, None] + band_shift[:, None, None] - positions[None, None, :]
    weights = tap_weights(sub_phase)
    matrix = jnp.zeros(whole.shape, sub_phase.dtype)
    for tap in range(TAPS):
        matrix = jnp.where(whole == tap - 3, weights[:, tap][:, None, None], matrix)
    return matrix


def warp_batch(slab_images, row_shift, col_shift, row_phase, col_phase):
    side_len = slab_images.shape[1]
    left_matrix = lanczos_batch(row_shift, row_phase, side_len)
    middle = jnp.einsum("kia,kab->kib", left_matrix, slab_images, precision=warp_mode)
    right_matrix = lanczos_batch(col_shift, col_phase, side_len)
    return jnp.einsum("kib,kjb->kij", middle, right_matrix, precision=warp_mode)


def chebyshev_rows(first_pixel, side_len):
    pixels = (first_pixel + jnp.arange(side_len, dtype=jnp.int32)).astype(jnp.float32)
    coordinate = (2.0 * pixels + 1.0) / TILE - 1.0
    orders = jnp.arange(TERMS, dtype=jnp.int32).astype(jnp.float32)
    return jnp.cos(orders[:, None] * jnp.arccos(coordinate)[None, :])


def basis_pair(anchor_pairs, side_len):
    row_basis = jax.vmap(lambda first_pixel: chebyshev_rows(first_pixel, side_len))(
        anchor_pairs[:, 0]
    )
    col_basis = jax.vmap(lambda first_pixel: chebyshev_rows(first_pixel, side_len))(
        anchor_pairs[:, 1]
    )
    return (row_basis, col_basis)


def project_terms(differences, row_basis, col_basis):
    middle = jnp.einsum("mtp,mpq->mtq", row_basis, differences, precision=warp_mode)
    return jnp.einsum("mtq,muq->mtu", middle, col_basis, precision=exact_mode)


BASIS_ROWS = 24


def reference_terms_kernel(patch_of, ref_ref, row_ref, col_ref, out_ref):
    image = ref_ref[0]
    rows_high = row_ref[0, 0]
    rows_low = row_ref[0, 1]
    image_high = image.astype(jnp.bfloat16)
    image_low = (image - image_high.astype(jnp.float32)).astype(jnp.bfloat16)
    middle = jnp.dot(rows_high, image_high, preferred_element_type=jnp.float32)
    middle = middle + jnp.dot(rows_low, image_high, preferred_element_type=jnp.float32)
    middle = middle + jnp.dot(rows_high, image_low, preferred_element_type=jnp.float32)
    out_ref[0] = lax.dot_general(
        middle, col_ref[0], (((1,), (1,)), ((), ())), preferred_element_type=jnp.float32, precision=exact_mode
    )


def reference_terms(ref_block, piece_patch, row_basis, col_basis):
    piece_count, terms, side_len = row_basis.shape
    pad = ((0, 0), (0, BASIS_ROWS - terms), (0, 0))
    padded_rows = jnp.pad(row_basis, pad)
    rows_high = padded_rows.astype(jnp.bfloat16)
    rows_low = (padded_rows - rows_high.astype(jnp.float32)).astype(jnp.bfloat16)
    rows = jnp.stack([rows_high, rows_low], axis=1)
    cols = jnp.pad(col_basis, pad)
    basis_spec = pl.BlockSpec((1, BASIS_ROWS, side_len), lambda k, patch_of: (k, 0, 0))
    out = pl.pallas_call(
        reference_terms_kernel,
        out_shape=jax.ShapeDtypeStruct((piece_count, BASIS_ROWS, BASIS_ROWS), jnp.float32),
        grid_spec=pltpu.PrefetchScalarGridSpec(
            num_scalar_prefetch=1,
            grid=(piece_count,),
            in_specs=[
                pl.BlockSpec((1, side_len, side_len), lambda k, patch_of: (patch_of[k], 0, 0)),
                pl.BlockSpec((1, 2, BASIS_ROWS, side_len), lambda k, patch_of: (k, 0, 0, 0)),
                basis_spec,
            ],
            out_specs=pl.BlockSpec((1, BASIS_ROWS, BASIS_ROWS), lambda k, patch_of: (k, 0, 0)),
        ),
        cost_estimate=pl.CostEstimate(
            flops=2 * piece_count * BASIS_ROWS * side_len * (side_len + BASIS_ROWS),
            bytes_accessed=4 * piece_count * side_len * (side_len + 2 * BASIS_ROWS),
            transcendentals=0,
        ),
    )(piece_patch, ref_block, rows, cols)
    return out[:, :terms, :terms]


def matched_kernel(patch_of, warped_ref, ref_ref, rows_ref, coef_ref, col_ref, out_ref):
    middle = jnp.dot(rows_ref[0], coef_ref[0], preferred_element_type=jnp.float32, precision=exact_mode)
    cols = col_ref[0]
    middle_high = middle.astype(jnp.bfloat16)
    middle_low = (middle - middle_high.astype(jnp.float32)).astype(jnp.bfloat16)
    cols_high = cols.astype(jnp.bfloat16)
    cols_low = (cols - cols_high.astype(jnp.float32)).astype(jnp.bfloat16)
    fitted = jnp.dot(middle_high, cols_high, preferred_element_type=jnp.float32)
    fitted = fitted + jnp.dot(middle_low, cols_high, preferred_element_type=jnp.float32)
    fitted = fitted + jnp.dot(middle_high, cols_low, preferred_element_type=jnp.float32)
    out_ref[0] = (warped_ref[0] - ref_ref[0]) - fitted


def matched_pieces(warped_all, ref_block, piece_patch, row_basis, chosen, col_basis):
    piece_count, terms, side_len = row_basis.shape
    extra = BASIS_ROWS - terms
    rows = jnp.pad(jnp.transpose(row_basis, (0, 2, 1)), ((0, 0), (0, 0), (0, extra)))
    coefs = jnp.pad(chosen, ((0, 0), (0, extra), (0, extra)))
    cols = jnp.pad(col_basis, ((0, 0), (0, extra), (0, 0)))
    image_spec = pl.BlockSpec((1, side_len, side_len), lambda k, patch_of: (k, 0, 0))
    return pl.pallas_call(
        matched_kernel,
        out_shape=jax.ShapeDtypeStruct(warped_all.shape, jnp.float32),
        grid_spec=pltpu.PrefetchScalarGridSpec(
            num_scalar_prefetch=1,
            grid=(piece_count,),
            in_specs=[
                image_spec,
                pl.BlockSpec((1, side_len, side_len), lambda k, patch_of: (patch_of[k], 0, 0)),
                pl.BlockSpec((1, side_len, BASIS_ROWS), lambda k, patch_of: (k, 0, 0)),
                pl.BlockSpec((1, BASIS_ROWS, BASIS_ROWS), lambda k, patch_of: (k, 0, 0)),
                pl.BlockSpec((1, BASIS_ROWS, side_len), lambda k, patch_of: (k, 0, 0)),
            ],
            out_specs=image_spec,
        ),
        cost_estimate=pl.CostEstimate(
            flops=2 * piece_count * side_len * BASIS_ROWS * (side_len + BASIS_ROWS),
            bytes_accessed=12 * piece_count * side_len * side_len,
            transcendentals=0,
        ),
    )(piece_patch, warped_all, ref_block, rows, coefs, cols)


def ring_sum(value, axis_name):
    count = lax.axis_size(axis_name)
    me = lax.axis_index(axis_name)
    received = [value]
    for step in range(1, count):
        pairs = [(i, (i + step) % count) for i in range(count)]
        received.append(lax.ppermute(value, axis_name, pairs))
    stacked = jnp.stack(received)
    total = None
    for source in range(count):
        term = lax.dynamic_index_in_dim(stacked, (me - source) % count, 0, keepdims=False)
        total = term if total is None else total + term
    return total


def body(pieces, ref_patch, piece_patch, piece_visit, anchors, shifts, phases):
    piece_count = pieces.shape[0]
    side_len = pieces.shape[1]
    patch_count = lax.axis_size(PATCH_PARTS)
    gathered = lax.all_gather(ref_patch, PATCH_PARTS + VISIT_PARTS, axis=0, tiled=True)
    ref_block = gathered.reshape(patch_count, side_len, side_len)
    visit_slots = jnp.arange(VIS_DEV, dtype=jnp.int32)
    own_onehot = (piece_visit[:, None] == visit_slots[None, :]).astype(jnp.float32)
    warped_all = warp_batch(pieces, shifts[:, 0], shifts[:, 1], phases[:, 0], phases[:, 1])
    warped_all = lax.optimization_barrier(warped_all)
    row_basis, col_basis = basis_pair(anchors, side_len)
    warp_terms = project_terms(warped_all, row_basis, col_basis)
    ref_terms = reference_terms(ref_block, piece_patch, row_basis, col_basis)
    partial_value = warp_terms - ref_terms
    local_sums = jnp.einsum("kv,ktu->vtu", own_onehot, partial_value, precision=exact_mode)
    totals = ring_sum(ring_sum(local_sums, "pz"), "px")
    coefficients = totals / float(patch_count * (piece_count // VIS_DEV) * side_len * side_len)
    chosen = jnp.take(coefficients, piece_visit, axis=0)
    matched = matched_pieces(warped_all, ref_block, piece_patch, row_basis, chosen, col_basis)
    return (matched, coefficients)


def solution(mesh):
    visit_size = mesh.shape["visit"]
    patch_size = mesh.shape["patch"]
    fine = Mesh(
        mesh.devices.reshape(visit_size // 2, 2, 4, patch_size // 4),
        PIECE_AXES,
    )
    return jax.shard_map(
        body,
        mesh=fine,
        in_specs=(
            P(PIECE_AXES, None, None),
            P(PATCH_PARTS, VISIT_PARTS, None),
            P(PIECE_AXES),
            P(PIECE_AXES),
            P(PIECE_AXES, None),
            P(PIECE_AXES, None),
            P(PIECE_AXES, None),
        ),
        out_specs=(P(PIECE_AXES, None, None), P(VISIT_PARTS, None, None)),
        check_vma=False,
    )
```
